128 devices in a mesh: shot: 8 (over y, core), blk: 16 (over z, x).
Axes of the slice: x: 4, y: 4, z: 4, core: 2. Of those that a mesh axis runs over, the one named last changes fastest.
Arguments:
- model_blocks: bfloat16 [16384, 2, 4, 128], P(('shot', 'blk')), may hold values from 0.19921875 to 0.3984375
- block_scales: bfloat16 [16384], P(('shot', 'blk')), may hold values from 0.75 to 1.09375
- aperture_owner: int32 [16384, 1], replicated, may hold values from 0 to 127; in each aligned block of 128 rows (0 to 127, 128 to 255, ...) at most 2 rows name the same one
- aperture_local: int32 [16384], replicated, may hold values from 0 to 127
- source_cell: int32 [8], P('shot'), may hold values from 0 to 2097151
- wavelet: float32 [8, 8], P('shot'), may hold values from -6 to 6
- receiver_cell: int32 [8, 16, 128], P('shot', 'blk'), may hold values from 0 to 131071
- observed: float32 [8, 16, 8, 128], P('shot', 'blk'), may hold values from -6 to 6
- field_now: float32 [8, 512, 32, 128], P('shot', 'blk'), may hold values from -6 to 6
- field_change: float32 [8, 512, 32, 128], P('shot', 'blk'), may hold values from -1.5 to 1.5
- adjoint_last: float32 [8, 512, 32, 128], P('shot', 'blk'), may hold values from -6 to 6
- adjoint_change: float32 [8, 512, 32, 128], P('shot', 'blk'), may hold values from -1.5 to 1.5
Outputs:
- gradient: float32 [16384, 2, 4, 128], P(('shot', 'blk'))
- field_end: float32 [8, 512, 32, 128], P('shot', 'blk')
- adjoint_first: float32 [8, 512, 32, 128], P('shot', 'blk')
The draws below stay inside these ranges and needn't reach their ends.
Inputs may be any that keep to these rules, and one draw needn't show every extreme that they name: `aperture_owner`: among the 128 rows of one device no owner appears more than 2 times, and some owner appears exactly 2 times.
All inputs are finite; a program needn't handle non-finite values.
Results may differ from the reference program's by a relative error of at most 0.0015.
Values may be sent and summed in bfloat16 or wider, within the bound.
No kernel may reach another device: no remote copies, remote signals or barrier semaphores. Data moves between devices by JAX's collectives and lax.ppermute only.
A program may use at most 64 MiB of HBM per device.

```python
import math
import jax
import jax.numpy as jnp
import numpy as np

BX = 2
BY = 4
BZ = 128
KX = 16
KY = 8
OWN_DEV = 128
STEPS = 8
NREC = 128
K = 128
CAP = 2
PX = 32
PY = 32
SX = 512
NBLOCKS = 16384
N_SHOT = 8
N_BLK = 16
DEVICES = 128


def plant(drawn, own_key, low, largest):
    place = [jax.random.randint(jax.random.fold_in(own_key, axis), (), 0, length) for axis, length in enumerate(drawn.shape)]
    widest = drawn.shape.index(max(drawn.shape))
    beside = place[:widest] + [(place[widest] + 1) % drawn.shape[widest]] + place[widest + 1:]
    return drawn.at[tuple(place)].set(low).at[tuple(beside)].set(largest)


def steps_of(key, shape, split, least, largest):
    level, own = 1.0, jax.random.fold_in(key, 6)
    for axis_at, parts in split:
        heights = jnp.exp(jax.random.uniform(jax.random.fold_in(own, axis_at), (parts,), jnp.float32, least / len(split), largest / len(split)))
        level = level * jnp.repeat(heights, shape[axis_at] // parts).reshape([-1 if axis == axis_at else 1 for axis in range(len(shape))])
    return level


def deal_out(key, own, number, rows, number_of, top, limit, skew):
    order = jax.random.permutation(key, number_of)
    heavy_load, usual = load_shares(number_of, rows * top, limit, skew, True), load_shares(number_of, rows * top, limit, skew, False)
    places = jnp.arange(number_of)

    def named(tallies, offset_by):
        used = int((tallies > 0).sum())
        fixed = max(1, used // 4)
        moved = fixed + (places - fixed + offset_by * (used - fixed)) % max(1, number_of - fixed)
        return jnp.zeros((number_of,), jnp.int32).at[order[jnp.where(places < fixed, places, moved)]].set(jnp.asarray(tallies, jnp.int32))

    tallies = jnp.where(number % 4 == 0, named(heavy_load, number // 4), named(usual, number - number // 4 - 1))
    mixed = jax.random.permutation(jax.random.fold_in(own, 3), number_of)
    source_of, receiver = mixed[0:number_of // 2 * 2:2], mixed[1:number_of // 2 * 2:2]
    room = jnp.minimum(tallies[source_of] - 1, limit - tallies[receiver]) // 2
    room = jnp.where((source_of == order[0]) | (receiver == order[0]) | (tallies[receiver] == 0), 0, jnp.maximum(room, 0))
    moved = jax.random.randint(jax.random.fold_in(own, 4), (number_of // 2,), 0, 1 << 20) % (room + 1)
    tallies = tallies.at[source_of].add(-moved).at[receiver].add(moved)
    items = jnp.searchsorted(jnp.cumsum(tallies), jnp.arange(rows * top), side="right").astype(jnp.int32)
    table = items.reshape(top, rows).T
    table = table[jax.random.permutation(jax.random.fold_in(own, 1), rows)]
    offset_by = jax.random.randint(jax.random.fold_in(own, 2), (rows, 1), 0, top)
    return jnp.take_along_axis(table, (jnp.arange(top)[None, :] + offset_by) % top, axis=1)


def load_shares(count, total, reach, skew, full):
    portions = [(1 << 20) // math.isqrt(rank ** skew) + 1 for rank in range(1, count + 1)]
    largest = reach if full else min(reach, max(-(-total // count), total * portions[0] // sum(portions)))
    least = 1 if total - largest >= count - 1 else 0
    given, rest = [largest] + [least] * (count - 1), total - largest - least * (count - 1)
    while rest > 0:
        free = [i for i in range(1, count) if given[i] < largest] or [i for i in range(1, count) if given[i] < reach]
        mass, remaining = sum([portions[i] for i in free]), rest
        for i in free:
            extra = min(reach - given[i], max(1, remaining * portions[i] // mass), rest)
            given[i] = given[i] + extra
            rest = rest - extra
    return np.array(given)


def scatter_about(stream_key, dims, width, bound, cuts=(), kind=jnp.bfloat16):
    drawn = jax.random.normal(stream_key, dims, jnp.float32) * width
    if len(cuts) > 0:
        drawn = steps_of(stream_key, dims, cuts, -0.22, 0.18) * drawn
    return jnp.clip(drawn, min=-bound, max=bound).astype(kind)


def setup_inputs(seed: int = 0) -> dict:
    seeds = jax.random.split(jax.random.key(seed), 13)
    model_blocks = jnp.clip(0.19921875 + 0.19921875 * jax.random.uniform(seeds[0], (NBLOCKS, BX, BY, BZ), jnp.float32) ** steps_of(seeds[0], (NBLOCKS, BX, BY, BZ), ((0, 128),), -0.2, 0.2), 0.19921875, 0.3984375).astype(jnp.bfloat16)
    block_scales = jnp.clip(jnp.exp(math.log(1.09375) - 0.37729423 * jax.random.uniform(seeds[1], (NBLOCKS,), jnp.float32) ** steps_of(seeds[1], (NBLOCKS,), ((0, 128),), -0.2, 0.2)), 0.75, 1.09375).astype(jnp.bfloat16)
    aperture_owner_keys = jax.random.split(jax.random.fold_in(seeds[2], 1), (DEVICES * K) // K)
    aperture_owner_turns = jax.random.permutation(jax.random.fold_in(seeds[2], 3), (DEVICES * K) // K)
    aperture_owner = jax.vmap(lambda own, number: deal_out(jax.random.fold_in(seeds[2], 2), own, number, K, DEVICES, 1, CAP, 2))(aperture_owner_keys, aperture_owner_turns).reshape((DEVICES * K, 1))
    aperture_local = plant(jax.random.randint(seeds[3], (DEVICES * K,), 0, OWN_DEV), jax.random.fold_in(seeds[3], 1), 0, OWN_DEV - 1).astype(jnp.int32)
    source_cell = plant(jax.random.randint(seeds[4], (N_SHOT,), 0, SX * PY * BZ), jax.random.fold_in(seeds[4], 1), 0, (SX * PY * BZ) - 1).astype(jnp.int32)
    wavelet = scatter_about(seeds[5], (N_SHOT, STEPS), 1.0, 6.0, ((0, 8),), jnp.float32)
    receiver_cell = plant(jax.random.randint(seeds[6], (N_SHOT, N_BLK, NREC), 0, PX * PY * BZ), jax.random.fold_in(seeds[6], 1), 0, (PX * PY * BZ) - 1).astype(jnp.int32)
    observed = scatter_about(seeds[7], (N_SHOT, N_BLK, STEPS, NREC), 1.0, 6.0, ((0, 8), (1, 16)), jnp.float32)
    field_now = scatter_about(seeds[8], (N_SHOT, SX, PY, BZ), 1.0, 6.0, ((0, 8), (1, 16)), jnp.float32)
    field_change = scatter_about(seeds[9], (N_SHOT, SX, PY, BZ), 0.25, 1.5, ((0, 8), (1, 16)), jnp.float32)
    adjoint_last = scatter_about(seeds[10], (N_SHOT, SX, PY, BZ), 1.0, 6.0, ((0, 8), (1, 16)), jnp.float32)
    adjoint_change = scatter_about(seeds[11], (N_SHOT, SX, PY, BZ), 0.25, 1.5, ((0, 8), (1, 16)), jnp.float32)
    return {"model_blocks": model_blocks, "block_scales": block_scales, "aperture_owner": aperture_owner, "aperture_local": aperture_local, "source_cell": source_cell, "wavelet": wavelet, "receiver_cell": receiver_cell, "observed": observed, "field_now": field_now, "field_change": field_change, "adjoint_last": adjoint_last, "adjoint_change": adjoint_change}


COEFFS = (-205.0 / 72.0, 8.0 / 5.0, -1.0 / 5.0, 8.0 / 315.0, -1.0 / 560.0)
GRADIENT_GAIN = 0.0625


def stencil(padded, extent):
    centre = padded[4:4 + extent[0], 4:4 + extent[1], 4:4 + extent[2]]
    summed = (3.0 * COEFFS[0]) * centre
    for offset in range(1, 5):
        beside_all = (padded[4 + offset:4 + offset + extent[0], 4:4 + extent[1], 4:4 + extent[2]]
                  + padded[4 - offset:4 - offset + extent[0], 4:4 + extent[1], 4:4 + extent[2]]
                  + padded[4:4 + extent[0], 4 + offset:4 + offset + extent[1], 4:4 + extent[2]]
                  + padded[4:4 + extent[0], 4 - offset:4 - offset + extent[1], 4:4 + extent[2]]
                  + padded[4:4 + extent[0], 4:4 + extent[1], 4 + offset:4 + offset + extent[2]]
                  + padded[4:4 + extent[0], 4:4 + extent[1], 4 - offset:4 - offset + extent[2]])
        summed = summed + COEFFS[offset] * beside_all
    return summed


def laplace(field):
    return stencil(jnp.pad(field, 4), field.shape)


def to_piece(blocks):
    return blocks.reshape(KX, KY, BX, BY, BZ).transpose(0, 2, 1, 3, 4).reshape(KX * BX, KY * BY, BZ)


def to_blocks(field_piece):
    return field_piece.reshape(KX, BX, KY, BY, BZ).transpose(0, 2, 1, 3, 4).reshape(KX * KY, BX, BY, BZ)


def reference(model_blocks, block_scales, aperture_owner, aperture_local, source_cell, wavelet, receiver_cell, observed, field_now, field_change, adjoint_last, adjoint_change):
    block_ids = (aperture_owner[:, 0] * OWN_DEV + aperture_local).astype(jnp.int32)
    values = model_blocks[block_ids].astype(jnp.float32) * block_scales[block_ids].astype(jnp.float32)[:, None, None, None]
    squared = values * values
    device_count = N_SHOT * N_BLK
    pieces = jax.vmap(to_piece)(squared.reshape(device_count, KX * KY, BX, BY, BZ))
    pieces = pieces.reshape(N_SHOT, N_BLK * KX * BX, KY * BY, BZ)
    piece_cells = KX * BX * KY * BY * BZ
    partial_list = []
    end_fields = []
    first_fields = []
    for shot_index in range(N_SHOT):
        courant = pieces[shot_index]
        offsets = jnp.arange(N_BLK, dtype=jnp.int32)[:, None] * piece_cells
        listen = (receiver_cell[shot_index] + offsets).reshape(-1)
        record = observed[shot_index].transpose(1, 0, 2).reshape(STEPS, N_BLK * NREC)
        current = field_now[shot_index]
        before = current - field_change[shot_index]
        snapshots = []
        misfit = []
        for step_index in range(STEPS):
            curved = laplace(current)
            snapshots.append(curved)
            advanced = 2.0 * current - before + courant * curved
            advanced = advanced.reshape(-1).at[source_cell[shot_index]].add(wavelet[shot_index, step_index]).reshape(advanced.shape)
            misfit.append(advanced.reshape(-1)[listen] - record[step_index])
            before = current
            current = advanced
        end_fields.append(current)
        adjoint_next = adjoint_last[shot_index]
        latest = adjoint_next - adjoint_change[shot_index]
        gradient_field = jnp.zeros_like(adjoint_next)
        for step_index in range(STEPS - 1, -1, -1):
            adjoint = 2.0 * adjoint_next - latest + laplace(courant * adjoint_next)
            adjoint = adjoint.reshape(-1).at[listen].add(misfit[step_index]).reshape(adjoint.shape)
            gradient_field = gradient_field + adjoint * snapshots[step_index]
            latest = adjoint_next
            adjoint_next = adjoint
        first_fields.append(adjoint_next)
        scaled_field = (GRADIENT_GAIN * gradient_field).reshape(N_BLK, KX * BX, KY * BY, BZ)
        partial_list.append(jax.vmap(to_blocks)(scaled_field).reshape(N_BLK * KX * KY, BX, BY, BZ))
    gradient = jax.ops.segment_sum(jnp.concatenate(partial_list, axis=0), block_ids, num_segments=NBLOCKS)
    return (gradient, jnp.stack(end_fields), jnp.stack(first_fields))
```

```python
import jax
import jax.numpy as jnp
from jax import lax
from jax.sharding import PartitionSpec as P

BX = 2
BY = 4
BZ = 128
KX = 16
KY = 8
STEPS = 8
GROUP = 4


COEFFS = (-205.0 / 72.0, 8.0 / 5.0, -1.0 / 5.0, 8.0 / 315.0, -1.0 / 560.0)
GRADIENT_GAIN = 0.0625


def from_left(x):
    count = lax.axis_size("blk")
    return lax.ppermute(x, "blk", [(i, i + 1) for i in range(count - 1)])


def from_right(x):
    count = lax.axis_size("blk")
    return lax.ppermute(x, "blk", [(i + 1, i) for i in range(count - 1)])


def extend(cells, width):
    if width == 0:
        return cells
    size = cells.shape[0]
    left = from_left(cells[size - width :])
    right = from_right(cells[:width])
    return jnp.concatenate([left, cells, right], axis=0)


def crop(cells, offset, want, own):
    start = offset - want
    return cells[start : start + own + 2 * want]


def lap_valid(cells):
    extent = (cells.shape[0] - 8, cells.shape[1], cells.shape[2])
    padded = jnp.pad(cells, ((0, 0), (4, 4), (4, 4)))
    centre = padded[4 : 4 + extent[0], 4 : 4 + extent[1], 4 : 4 + extent[2]]
    summed = 3.0 * COEFFS[0] * centre
    for offset in range(1, 5):
        beside_all = (
            padded[4 + offset : 4 + offset + extent[0], 4 : 4 + extent[1], 4 : 4 + extent[2]]
            + padded[4 - offset : 4 - offset + extent[0], 4 : 4 + extent[1], 4 : 4 + extent[2]]
            + padded[4 : 4 + extent[0], 4 + offset : 4 + offset + extent[1], 4 : 4 + extent[2]]
            + padded[4 : 4 + extent[0], 4 - offset : 4 - offset + extent[1], 4 : 4 + extent[2]]
            + padded[4 : 4 + extent[0], 4 : 4 + extent[1], 4 + offset : 4 + offset + extent[2]]
            + padded[4 : 4 + extent[0], 4 : 4 + extent[1], 4 - offset : 4 - offset + extent[2]]
        )
        summed = summed + COEFFS[offset] * beside_all
    return summed


def to_piece(blocks):
    return blocks.reshape(KX, KY, BX, BY, BZ).transpose(0, 2, 1, 3, 4).reshape(KX * BX, KY * BY, BZ)


def to_blocks(field_piece):
    return (
        field_piece.reshape(KX, BX, KY, BY, BZ)
        .transpose(0, 2, 1, 3, 4)
        .reshape(KX * KY, BX, BY, BZ)
    )


def local(
    model_blocks,
    block_scales,
    aperture_owner,
    aperture_local,
    source_cell,
    wavelet,
    receiver_cell,
    observed,
    field_now,
    field_change,
    adjoint_last,
    adjoint_change,
):
    devices_all = lax.axis_size(("shot", "blk"))
    my_index = lax.axis_index(("shot", "blk"))
    blk_index = lax.axis_index("blk")
    slot_count = aperture_local.shape[0] // devices_all
    cap_rows = 2
    halo = 4 * GROUP

    current = field_now[0]
    before = current - field_change[0]
    own, size_y, size_z = current.shape
    plane = size_y * size_z
    u_ext = extend(current, halo)
    b_ext = extend(before, halo - 4)
    adjoint_next = adjoint_last[0]
    latest = adjoint_next - adjoint_change[0]
    m_ext = extend(adjoint_next, halo)
    l_ext = extend(latest, halo - 4)
    listen = receiver_cell[0, 0]
    listen_left = from_left(listen)
    listen_right = from_right(listen)

    owner_table = aperture_owner[:, 0].reshape(devices_all, slot_count)
    local_table = aperture_local.reshape(devices_all, slot_count)
    picked = owner_table == my_index
    count = jnp.sum(picked.astype(jnp.int32), axis=1)
    first = jnp.argmax(picked, axis=1)
    last = slot_count - 1 - jnp.argmax(picked[:, ::-1], axis=1)
    lookup = jnp.stack(
        [
            jnp.take_along_axis(local_table, first[:, None], axis=1)[:, 0],
            jnp.take_along_axis(local_table, last[:, None], axis=1)[:, 0],
        ],
        axis=1,
    )
    filled = jnp.stack([count >= 1, count >= 2], axis=1)
    block_shape = model_blocks.shape[1:]
    block_rows = BX * BY
    outgoing = jnp.where(
        filled[:, :, None, None], model_blocks[lookup].reshape(devices_all, cap_rows, block_rows, BZ),
        jnp.zeros((), model_blocks.dtype),
    )
    out_scales = jnp.where(filled, block_scales[lookup], jnp.zeros((), block_scales.dtype))
    payload = jnp.concatenate(
        [outgoing, jnp.broadcast_to(out_scales[:, :, None, None], (devices_all, cap_rows, 1, BZ))], axis=2
    )
    arrived = lax.all_to_all(payload, ("shot", "blk"), split_axis=0, concat_axis=0, tiled=True)

    my_owners = lax.dynamic_index_in_dim(owner_table, my_index, 0, keepdims=False)
    earlier = jnp.arange(slot_count)[None, :] < jnp.arange(slot_count)[:, None]
    my_ranks = jnp.sum(
        jnp.logical_and(my_owners[:, None] == my_owners[None, :], earlier).astype(jnp.int32), axis=1
    )
    flat_slot = my_owners * cap_rows + my_ranks
    rows = arrived.reshape(devices_all * cap_rows, block_rows + 1, BZ)[flat_slot]
    values = rows[:, :block_rows].reshape((slot_count,) + block_shape).astype(jnp.float32)
    gain_rows = rows[:, block_rows, 0].astype(jnp.float32)
    scaled = values * gain_rows[:, None, None, None]
    courant = to_piece(scaled * scaled)
    c_ext = extend(courant, halo)

    source_x = source_cell[0] // plane - blk_index * own
    source_rest = source_cell[0] % plane
    record = observed[0, 0]

    snapshots = []
    misfit = []
    u_off, b_off = halo, halo - 4
    for step_index in range(STEPS):
        if step_index > 0 and step_index % GROUP == 0:
            u_own = crop(u_ext, u_off, 0, own)
            b_own = crop(b_ext, b_off, 0, own)
            u_ext, u_off = extend(u_own, halo), halo
            b_ext, b_off = extend(b_own, halo - 4), halo - 4
        new_off = u_off - 4
        curved = lap_valid(u_ext)
        snapshots.append(crop(curved, new_off, 0, own))
        advanced = (
            2.0 * crop(u_ext, u_off, new_off, own)
            - crop(b_ext, b_off, new_off, own)
            + crop(c_ext, halo, new_off, own) * curved
        )
        ext_x = source_x + new_off
        inside = jnp.logical_and(ext_x >= 0, ext_x < own + 2 * new_off)
        spot = jnp.clip(ext_x, 0, own + 2 * new_off - 1) * plane + source_rest
        amount = jnp.where(inside, wavelet[0, step_index], jnp.zeros((), jnp.float32))
        shape_now = advanced.shape
        advanced = advanced.reshape(-1).at[spot].add(amount).reshape(shape_now)
        misfit.append(crop(advanced, new_off, 0, own).reshape(-1)[listen] - record[step_index])
        b_ext, b_off = u_ext, u_off
        u_ext, u_off = advanced, new_off
    field_end = crop(u_ext, u_off, 0, own)

    misfit_all = jnp.stack(misfit)
    misfit_ext = jnp.concatenate([from_left(misfit_all), misfit_all, from_right(misfit_all)], axis=1)
    cells_all = jnp.concatenate([listen_left, listen, listen_right])
    shift_all = jnp.concatenate(
        [
            jnp.full(listen.shape, -own, jnp.int32),
            jnp.zeros(listen.shape, jnp.int32),
            jnp.full(listen.shape, own, jnp.int32),
        ]
    )
    rec_x = cells_all // plane + shift_all
    rec_rest = cells_all % plane

    m_off, l_off = halo, halo - 4
    gradient_field = jnp.zeros_like(adjoint_next)
    for count_index, step_index in enumerate(range(STEPS - 1, -1, -1)):
        if count_index > 0 and count_index % GROUP == 0:
            m_own = crop(m_ext, m_off, 0, own)
            l_own = crop(l_ext, l_off, 0, own)
            m_ext, m_off = extend(m_own, halo), halo
            l_ext, l_off = extend(l_own, halo - 4), halo - 4
        new_off = m_off - 4
        adjoint = (
            2.0 * crop(m_ext, m_off, new_off, own)
            - crop(l_ext, l_off, new_off, own)
            + lap_valid(crop(c_ext, halo, m_off, own) * m_ext)
        )
        ext_x = rec_x + new_off
        valid = jnp.logical_and(ext_x >= 0, ext_x < own + 2 * new_off)
        spots = jnp.clip(ext_x, 0, own + 2 * new_off - 1) * plane + rec_rest
        amounts = jnp.where(valid, misfit_ext[step_index], jnp.zeros((), jnp.float32))
        shape_now = adjoint.shape
        adjoint = adjoint.reshape(-1).at[spots].add(amounts).reshape(shape_now)
        gradient_field = gradient_field + crop(adjoint, new_off, 0, own) * snapshots[step_index]
        l_ext, l_off = m_ext, m_off
        m_ext, m_off = adjoint, new_off
    adjoint_first = crop(m_ext, m_off, 0, own)

    partial_blocks = to_blocks(GRADIENT_GAIN * gradient_field)
    pair_count = devices_all * cap_rows
    slot_for = jnp.zeros((pair_count,), jnp.int32).at[flat_slot].set(jnp.arange(slot_count, dtype=jnp.int32))
    has = jnp.zeros((pair_count,), jnp.bool_).at[flat_slot].set(True)
    parcel = jnp.where(has[:, None, None, None], partial_blocks[slot_for], jnp.zeros((), jnp.float32))
    parcel = parcel.reshape((devices_all, cap_rows) + block_shape)
    returned = lax.all_to_all(parcel, ("shot", "blk"), split_axis=0, concat_axis=0, tiled=True)
    owned_count = model_blocks.shape[0]
    chooser = jnp.logical_and(
        lookup.reshape(-1)[None, :] == jnp.arange(owned_count, dtype=lookup.dtype)[:, None],
        filled.reshape(-1)[None, :],
    ).astype(jnp.float32)
    gradient = jnp.dot(
        chooser,
        returned.reshape(pair_count, -1),
        precision=lax.Precision.HIGHEST,
        preferred_element_type=jnp.float32,
    ).reshape(model_blocks.shape)
    return (gradient, field_end[None], adjoint_first[None])


def solution(mesh):
    in_specs = (
        P(("shot", "blk"), None, None, None),
        P(("shot", "blk")),
        P(),
        P(),
        P("shot"),
        P("shot", None),
        P("shot", "blk", None),
        P("shot", "blk", None, None),
        P("shot", "blk", None, None),
        P("shot", "blk", None, None),
        P("shot", "blk", None, None),
        P("shot", "blk", None, None),
    )
    out_specs = (
        P(("shot", "blk"), None, None, None),
        P("shot", "blk", None, None),
        P("shot", "blk", None, None),
    )
    return jax.shard_map(local, mesh=mesh, in_specs=in_specs, out_specs=out_specs, check_vma=False)
```

```python
import jax
import jax.numpy as jnp
from jax import lax
from jax.sharding import PartitionSpec as P

BX = 2
BY = 4
BZ = 128
KX = 16
KY = 8
STEPS = 8
GROUP = 4


COEFFS = (-205.0 / 72.0, 8.0 / 5.0, -1.0 / 5.0, 8.0 / 315.0, -1.0 / 560.0)
GRADIENT_GAIN = 0.0625


def from_left(x):
    count = lax.axis_size("blk")
    return lax.ppermute(x, "blk", [(i, i + 1) for i in range(count - 1)])


def from_right(x):
    count = lax.axis_size("blk")
    return lax.ppermute(x, "blk", [(i + 1, i) for i in range(count - 1)])


def pack(parts):
    return jnp.concatenate([part.reshape(-1, part.shape[-1]) for part in parts], axis=0)


def unpack(buffer, likes):
    pieces, start = [], 0
    for like in likes:
        rows = like.size // like.shape[-1]
        pieces.append(buffer[start : start + rows].reshape(like.shape))
        start += rows
    return pieces


def swap(to_right, to_left):
    got_left = unpack(from_left(pack(to_right)), to_right)
    got_right = unpack(from_right(pack(to_left)), to_left)
    return got_left, got_right


def extend_all(fields):
    tails = [cells[cells.shape[0] - width :] for cells, width in fields]
    heads = [cells[:width] for cells, width in fields]
    got_left, got_right = swap(tails, heads)
    return [
        jnp.concatenate([left, cells, right], axis=0)
        for (cells, _), left, right in zip(fields, got_left, got_right)
    ]


def crop(cells, offset, want, own):
    start = offset - want
    return cells[start : start + own + 2 * want]


def lap_valid(cells):
    extent = (cells.shape[0] - 8, cells.shape[1], cells.shape[2])
    padded = jnp.pad(cells, ((0, 0), (4, 4), (4, 4)))
    centre = padded[4 : 4 + extent[0], 4 : 4 + extent[1], 4 : 4 + extent[2]]
    summed = 3.0 * COEFFS[0] * centre
    for offset in range(1, 5):
        beside_all = (
            padded[4 + offset : 4 + offset + extent[0], 4 : 4 + extent[1], 4 : 4 + extent[2]]
            + padded[4 - offset : 4 - offset + extent[0], 4 : 4 + extent[1], 4 : 4 + extent[2]]
            + padded[4 : 4 + extent[0], 4 + offset : 4 + offset + extent[1], 4 : 4 + extent[2]]
            + padded[4 : 4 + extent[0], 4 - offset : 4 - offset + extent[1], 4 : 4 + extent[2]]
            + padded[4 : 4 + extent[0], 4 : 4 + extent[1], 4 + offset : 4 + offset + extent[2]]
            + padded[4 : 4 + extent[0], 4 : 4 + extent[1], 4 - offset : 4 - offset + extent[2]]
        )
        summed = summed + COEFFS[offset] * beside_all
    return summed


def to_piece(blocks):
    return blocks.reshape(KX, KY, BX, BY, BZ).transpose(0, 2, 1, 3, 4).reshape(KX * BX, KY * BY, BZ)


def to_blocks(field_piece):
    return (
        field_piece.reshape(KX, BX, KY, BY, BZ)
        .transpose(0, 2, 1, 3, 4)
        .reshape(KX * KY, BX, BY, BZ)
    )


def one_hot_rows(index, count):
    return (index[:, None] == jnp.arange(count, dtype=index.dtype)[None, :]).astype(jnp.float32)


def exact_dot(left, right):
    return jnp.dot(left, right, precision=lax.Precision.HIGHEST, preferred_element_type=jnp.float32)


def local(
    model_blocks,
    block_scales,
    aperture_owner,
    aperture_local,
    source_cell,
    wavelet,
    receiver_cell,
    observed,
    field_now,
    field_change,
    adjoint_last,
    adjoint_change,
):
    devices_all = lax.axis_size(("shot", "blk"))
    my_index = lax.axis_index(("shot", "blk"))
    blk_index = lax.axis_index("blk")
    slot_count = aperture_local.shape[0] // devices_all
    cap_rows = 2
    halo = 4 * GROUP

    current = field_now[0]
    before = current - field_change[0]
    own, size_y, size_z = current.shape
    plane = size_y * size_z
    adjoint_next = adjoint_last[0]
    latest = adjoint_next - adjoint_change[0]
    listen = receiver_cell[0, 0]
    listen_row = listen.astype(jnp.float32)[None, :]
    first_fields = [(current, halo), (before, halo - 4), (adjoint_next, halo), (latest, halo - 4)]
    tails = [cells[own - width :] for cells, width in first_fields] + [listen_row]
    heads = [cells[:width] for cells, width in first_fields] + [listen_row]
    got_left, got_right = swap(tails, heads)
    u_ext, b_ext, m_ext, l_ext = [
        jnp.concatenate([left, cells, right], axis=0)
        for (cells, _), left, right in zip(first_fields, got_left, got_right)
    ]
    listen_left = got_left[-1][0].astype(jnp.int32)
    listen_right = got_right[-1][0].astype(jnp.int32)

    owner_table = aperture_owner[:, 0].reshape(devices_all, slot_count)
    local_table = aperture_local.reshape(devices_all, slot_count)
    picked = owner_table == my_index
    count = jnp.sum(picked.astype(jnp.int32), axis=1)
    first = jnp.argmax(picked, axis=1)
    last = slot_count - 1 - jnp.argmax(picked[:, ::-1], axis=1)
    lookup = jnp.stack(
        [
            jnp.take_along_axis(local_table, first[:, None], axis=1)[:, 0],
            jnp.take_along_axis(local_table, last[:, None], axis=1)[:, 0],
        ],
        axis=1,
    )
    filled = jnp.stack([count >= 1, count >= 2], axis=1)
    block_shape = model_blocks.shape[1:]
    block_rows = BX * BY
    outgoing = jnp.where(
        filled[:, :, None, None], model_blocks[lookup].reshape(devices_all, cap_rows, block_rows, BZ),
        jnp.zeros((), model_blocks.dtype),
    )
    out_scales = jnp.where(filled, block_scales[lookup], jnp.zeros((), block_scales.dtype))
    payload = jnp.concatenate(
        [outgoing, jnp.broadcast_to(out_scales[:, :, None, None], (devices_all, cap_rows, 1, BZ))], axis=2
    )
    arrived = lax.all_to_all(payload, ("shot", "blk"), split_axis=0, concat_axis=0, tiled=True)

    my_owners = lax.dynamic_index_in_dim(owner_table, my_index, 0, keepdims=False)
    earlier = jnp.arange(slot_count)[None, :] < jnp.arange(slot_count)[:, None]
    my_ranks = jnp.sum(
        jnp.logical_and(my_owners[:, None] == my_owners[None, :], earlier).astype(jnp.int32), axis=1
    )
    flat_slot = my_owners * cap_rows + my_ranks
    rows = arrived.reshape(devices_all * cap_rows, block_rows + 1, BZ)[flat_slot]
    values = rows[:, :block_rows].reshape((slot_count,) + block_shape).astype(jnp.float32)
    gain_rows = rows[:, block_rows, 0].astype(jnp.float32)
    scaled = values * gain_rows[:, None, None, None]
    courant = to_piece(scaled * scaled)
    (c_ext,) = extend_all([(courant, halo)])

    source_x = source_cell[0] // plane - blk_index * own
    source_rest = source_cell[0] % plane
    source_y = source_rest // size_z
    source_z = source_rest % size_z
    record = observed[0, 0]
    own_pick = one_hot_rows(listen // size_z, own * size_y)
    own_z = one_hot_rows(listen % size_z, size_z)

    snapshots = []
    misfit = []
    u_off, b_off = halo, halo - 4
    for step_index in range(STEPS):
        if step_index > 0 and step_index % GROUP == 0:
            u_ext, b_ext = extend_all([(crop(u_ext, u_off, 0, own), halo), (crop(b_ext, b_off, 0, own), halo - 4)])
            u_off, b_off = halo, halo - 4
        new_off = u_off - 4
        curved = lap_valid(u_ext)
        snapshots.append(crop(curved, new_off, 0, own))
        advanced = (
            2.0 * crop(u_ext, u_off, new_off, own)
            - crop(b_ext, b_off, new_off, own)
            + crop(c_ext, halo, new_off, own) * curved
        )
        shape_now = advanced.shape
        at_source = (
            (lax.broadcasted_iota(jnp.int32, shape_now, 0) == source_x + new_off)
            & (lax.broadcasted_iota(jnp.int32, shape_now, 1) == source_y)
            & (lax.broadcasted_iota(jnp.int32, shape_now, 2) == source_z)
        )
        advanced = advanced + jnp.where(at_source, wavelet[0, step_index], jnp.zeros((), jnp.float32))
        sampled = exact_dot(own_pick, crop(advanced, new_off, 0, own).reshape(own * size_y, size_z))
        misfit.append(jnp.sum(sampled * own_z, axis=1) - record[step_index])
        b_ext, b_off = u_ext, u_off
        u_ext, u_off = advanced, new_off
    field_end = crop(u_ext, u_off, 0, own)

    misfit_all = jnp.stack(misfit)
    (misfit_left,), (misfit_right,) = swap([misfit_all], [misfit_all])
    misfit_ext = jnp.concatenate([misfit_left, misfit_all, misfit_right], axis=1)
    cells_all = jnp.concatenate([listen_left, listen, listen_right])
    shift_all = jnp.concatenate(
        [
            jnp.full(listen.shape, -own, jnp.int32),
            jnp.zeros(listen.shape, jnp.int32),
            jnp.full(listen.shape, own, jnp.int32),
        ]
    )
    rec_x = cells_all // plane + shift_all + halo
    rec_plane = jnp.where(
        jnp.logical_and(rec_x >= 0, rec_x < own + 2 * halo), rec_x * size_y + (cells_all % plane) // size_z, -1
    )
    rec_pick = (
        jnp.arange((own + 2 * halo) * size_y, dtype=jnp.int32)[:, None] == rec_plane[None, :]
    ).astype(jnp.float32)
    rec_z = one_hot_rows(cells_all % size_z, size_z)

    m_off, l_off = halo, halo - 4
    gradient_field = jnp.zeros_like(adjoint_next)
    for count_index, step_index in enumerate(range(STEPS - 1, -1, -1)):
        if count_index > 0 and count_index % GROUP == 0:
            m_ext, l_ext = extend_all([(crop(m_ext, m_off, 0, own), halo), (crop(l_ext, l_off, 0, own), halo - 4)])
            m_off, l_off = halo, halo - 4
        new_off = m_off - 4
        adjoint = (
            2.0 * crop(m_ext, m_off, new_off, own)
            - crop(l_ext, l_off, new_off, own)
            + lap_valid(crop(c_ext, halo, m_off, own) * m_ext)
        )
        shape_now = adjoint.shape
        first_row = (halo - new_off) * size_y
        pick_now = rec_pick[first_row : first_row + shape_now[0] * size_y]
        injected = exact_dot(pick_now, rec_z * misfit_ext[step_index][:, None])
        adjoint = adjoint + injected.reshape(shape_now)
        gradient_field = gradient_field + crop(adjoint, new_off, 0, own) * snapshots[step_index]
        l_ext, l_off = m_ext, m_off
        m_ext, m_off = adjoint, new_off
    adjoint_first = crop(m_ext, m_off, 0, own)

    partial_blocks = to_blocks(GRADIENT_GAIN * gradient_field).reshape(slot_count, block_rows, BZ)
    pair_count = devices_all * cap_rows
    slot_for = jnp.zeros((pair_count,), jnp.int32).at[flat_slot].set(jnp.arange(slot_count, dtype=jnp.int32))
    has = jnp.zeros((pair_count,), jnp.bool_).at[flat_slot].set(True)
    parcel = jnp.where(has[:, None, None], partial_blocks[slot_for], jnp.zeros((), jnp.float32))
    parcel = parcel.reshape(devices_all, cap_rows, block_rows, BZ)
    returned = lax.all_to_all(parcel, ("shot", "blk"), split_axis=0, concat_axis=0, tiled=True)
    owned_count = model_blocks.shape[0]
    chooser = jnp.logical_and(
        lookup.reshape(-1)[None, :] == jnp.arange(owned_count, dtype=lookup.dtype)[:, None],
        filled.reshape(-1)[None, :],
    ).astype(jnp.float32)
    gradient = exact_dot(chooser, returned.reshape(pair_count, -1)).reshape(model_blocks.shape)
    return (gradient, field_end[None], adjoint_first[None])


def solution(mesh):
    in_specs = (
        P(("shot", "blk"), None, None, None),
        P(("shot", "blk")),
        P(),
        P(),
        P("shot"),
        P("shot", None),
        P("shot", "blk", None),
        P("shot", "blk", None, None),
        P("shot", "blk", None, None),
        P("shot", "blk", None, None),
        P("shot", "blk", None, None),
        P("shot", "blk", None, None),
    )
    out_specs = (
        P(("shot", "blk"), None, None, None),
        P("shot", "blk", None, None),
        P("shot", "blk", None, None),
    )
    return jax.shard_map(local, mesh=mesh, in_specs=in_specs, out_specs=out_specs, check_vma=False)
```

```python
import jax
import jax.numpy as jnp
from jax import lax
from jax.sharding import PartitionSpec as P

BX = 2
BY = 4
BZ = 128
KX = 16
KY = 8
STEPS = 8
GROUP = 8


COEFFS = (-205.0 / 72.0, 8.0 / 5.0, -1.0 / 5.0, 8.0 / 315.0, -1.0 / 560.0)
GRADIENT_GAIN = 0.0625


def from_left(x):
    count = lax.axis_size("blk")
    return lax.ppermute(x, "blk", [(i, i + 1) for i in range(count - 1)])


def from_right(x):
    count = lax.axis_size("blk")
    return lax.ppermute(x, "blk", [(i + 1, i) for i in range(count - 1)])


def pack(parts):
    return jnp.concatenate([part.reshape(-1, part.shape[-1]) for part in parts], axis=0)


def unpack(buffer, likes):
    pieces, start = [], 0
    for like in likes:
        rows = like.size // like.shape[-1]
        pieces.append(buffer[start : start + rows].reshape(like.shape))
        start += rows
    return pieces


def swap(to_right, to_left):
    got_left = unpack(from_left(pack(to_right)), to_right)
    got_right = unpack(from_right(pack(to_left)), to_left)
    return got_left, got_right


def extend_all(fields):
    tails = [cells[cells.shape[0] - width :] for cells, width in fields]
    heads = [cells[:width] for cells, width in fields]
    got_left, got_right = swap(tails, heads)
    return [
        jnp.concatenate([left, cells, right], axis=0)
        for (cells, _), left, right in zip(fields, got_left, got_right)
    ]


def crop(cells, offset, want, own):
    start = offset - want
    return cells[start : start + own + 2 * want]


def lap_valid(cells):
    extent = (cells.shape[0] - 8, cells.shape[1], cells.shape[2])
    padded = jnp.pad(cells, ((0, 0), (4, 4), (4, 4)))
    centre = padded[4 : 4 + extent[0], 4 : 4 + extent[1], 4 : 4 + extent[2]]
    summed = 3.0 * COEFFS[0] * centre
    for offset in range(1, 5):
        beside_all = (
            padded[4 + offset : 4 + offset + extent[0], 4 : 4 + extent[1], 4 : 4 + extent[2]]
            + padded[4 - offset : 4 - offset + extent[0], 4 : 4 + extent[1], 4 : 4 + extent[2]]
            + padded[4 : 4 + extent[0], 4 + offset : 4 + offset + extent[1], 4 : 4 + extent[2]]
            + padded[4 : 4 + extent[0], 4 - offset : 4 - offset + extent[1], 4 : 4 + extent[2]]
            + padded[4 : 4 + extent[0], 4 : 4 + extent[1], 4 + offset : 4 + offset + extent[2]]
            + padded[4 : 4 + extent[0], 4 : 4 + extent[1], 4 - offset : 4 - offset + extent[2]]
        )
        summed = summed + COEFFS[offset] * beside_all
    return summed


def to_piece(blocks):
    return blocks.reshape(KX, KY, BX, BY, BZ).transpose(0, 2, 1, 3, 4).reshape(KX * BX, KY * BY, BZ)


def to_blocks(field_piece):
    return (
        field_piece.reshape(KX, BX, KY, BY, BZ)
        .transpose(0, 2, 1, 3, 4)
        .reshape(KX * KY, BX, BY, BZ)
    )


def one_hot_rows(index, count):
    return (index[:, None] == jnp.arange(count, dtype=index.dtype)[None, :]).astype(jnp.float32)


def exact_dot(left, right):
    return jnp.dot(left, right, precision=lax.Precision.HIGHEST, preferred_element_type=jnp.float32)


def local(
    model_blocks,
    block_scales,
    aperture_owner,
    aperture_local,
    source_cell,
    wavelet,
    receiver_cell,
    observed,
    field_now,
    field_change,
    adjoint_last,
    adjoint_change,
):
    devices_all = lax.axis_size(("shot", "blk"))
    my_index = lax.axis_index(("shot", "blk"))
    blk_index = lax.axis_index("blk")
    slot_count = aperture_local.shape[0] // devices_all
    cap_rows = 2
    halo = 4 * GROUP

    current = field_now[0]
    before = current - field_change[0]
    own, size_y, size_z = current.shape
    plane = size_y * size_z
    adjoint_next = adjoint_last[0]
    latest = adjoint_next - adjoint_change[0]
    listen = receiver_cell[0, 0]
    listen_row = listen.astype(jnp.float32)[None, :]
    first_fields = [(current, halo), (before, halo - 4), (adjoint_next, halo), (latest, halo - 4)]
    tails = [cells[own - width :] for cells, width in first_fields] + [listen_row]
    heads = [cells[:width] for cells, width in first_fields] + [listen_row]
    got_left, got_right = swap(tails, heads)
    u_ext, b_ext, m_ext, l_ext = [
        jnp.concatenate([left, cells, right], axis=0)
        for (cells, _), left, right in zip(first_fields, got_left, got_right)
    ]
    listen_left = got_left[-1][0].astype(jnp.int32)
    listen_right = got_right[-1][0].astype(jnp.int32)

    owner_table = aperture_owner[:, 0].reshape(devices_all, slot_count)
    local_table = aperture_local.reshape(devices_all, slot_count)
    picked = owner_table == my_index
    count = jnp.sum(picked.astype(jnp.int32), axis=1)
    first = jnp.argmax(picked, axis=1)
    last = slot_count - 1 - jnp.argmax(picked[:, ::-1], axis=1)
    lookup = jnp.stack(
        [
            jnp.take_along_axis(local_table, first[:, None], axis=1)[:, 0],
            jnp.take_along_axis(local_table, last[:, None], axis=1)[:, 0],
        ],
        axis=1,
    )
    filled = jnp.stack([count >= 1, count >= 2], axis=1)
    block_shape = model_blocks.shape[1:]
    block_rows = BX * BY
    outgoing = jnp.where(
        filled[:, :, None, None], model_blocks[lookup].reshape(devices_all, cap_rows, block_rows, BZ),
        jnp.zeros((), model_blocks.dtype),
    )
    out_scales = jnp.where(filled, block_scales[lookup], jnp.zeros((), block_scales.dtype))
    payload = jnp.concatenate(
        [outgoing, jnp.broadcast_to(out_scales[:, :, None, None], (devices_all, cap_rows, 1, BZ))], axis=2
    )
    arrived = lax.all_to_all(payload, ("shot", "blk"), split_axis=0, concat_axis=0, tiled=True)

    my_owners = lax.dynamic_index_in_dim(owner_table, my_index, 0, keepdims=False)
    earlier = jnp.arange(slot_count)[None, :] < jnp.arange(slot_count)[:, None]
    my_ranks = jnp.sum(
        jnp.logical_and(my_owners[:, None] == my_owners[None, :], earlier).astype(jnp.int32), axis=1
    )
    flat_slot = my_owners * cap_rows + my_ranks
    rows = arrived.reshape(devices_all * cap_rows, block_rows + 1, BZ)[flat_slot]
    values = rows[:, :block_rows].reshape((slot_count,) + block_shape).astype(jnp.float32)
    gain_rows = rows[:, block_rows, 0].astype(jnp.float32)
    scaled = values * gain_rows[:, None, None, None]
    courant = to_piece(scaled * scaled)
    (c_ext,) = extend_all([(courant, halo)])

    source_x = source_cell[0] // plane - blk_index * own
    source_rest = source_cell[0] % plane
    source_y = source_rest // size_z
    source_z = source_rest % size_z
    record = observed[0, 0]
    own_pick = one_hot_rows(listen // size_z, own * size_y)
    own_z = one_hot_rows(listen % size_z, size_z)

    snapshots = []
    misfit = []
    u_off, b_off = halo, halo - 4
    for step_index in range(STEPS):
        if step_index > 0 and step_index % GROUP == 0:
            u_ext, b_ext = extend_all([(crop(u_ext, u_off, 0, own), halo), (crop(b_ext, b_off, 0, own), halo - 4)])
            u_off, b_off = halo, halo - 4
        new_off = u_off - 4
        curved = lap_valid(u_ext)
        snapshots.append(crop(curved, new_off, 0, own))
        advanced = (
            2.0 * crop(u_ext, u_off, new_off, own)
            - crop(b_ext, b_off, new_off, own)
            + crop(c_ext, halo, new_off, own) * curved
        )
        shape_now = advanced.shape
        at_source = (
            (lax.broadcasted_iota(jnp.int32, shape_now, 0) == source_x + new_off)
            & (lax.broadcasted_iota(jnp.int32, shape_now, 1) == source_y)
            & (lax.broadcasted_iota(jnp.int32, shape_now, 2) == source_z)
        )
        advanced = advanced + jnp.where(at_source, wavelet[0, step_index], jnp.zeros((), jnp.float32))
        sampled = exact_dot(own_pick, crop(advanced, new_off, 0, own).reshape(own * size_y, size_z))
        misfit.append(jnp.sum(sampled * own_z, axis=1) - record[step_index])
        b_ext, b_off = u_ext, u_off
        u_ext, u_off = advanced, new_off
    field_end = crop(u_ext, u_off, 0, own)

    misfit_all = jnp.stack(misfit)
    (misfit_left,), (misfit_right,) = swap([misfit_all], [misfit_all])
    misfit_ext = jnp.concatenate([misfit_left, misfit_all, misfit_right], axis=1)
    cells_all = jnp.concatenate([listen_left, listen, listen_right])
    shift_all = jnp.concatenate(
        [
            jnp.full(listen.shape, -own, jnp.int32),
            jnp.zeros(listen.shape, jnp.int32),
            jnp.full(listen.shape, own, jnp.int32),
        ]
    )
    rec_x = cells_all // plane + shift_all + halo
    rec_plane = jnp.where(
        jnp.logical_and(rec_x >= 0, rec_x < own + 2 * halo), rec_x * size_y + (cells_all % plane) // size_z, -1
    )
    rec_pick = (
        jnp.arange((own + 2 * halo) * size_y, dtype=jnp.int32)[:, None] == rec_plane[None, :]
    ).astype(jnp.float32)
    rec_z = one_hot_rows(cells_all % size_z, size_z)

    m_off, l_off = halo, halo - 4
    gradient_field = jnp.zeros_like(adjoint_next)
    for count_index, step_index in enumerate(range(STEPS - 1, -1, -1)):
        if count_index > 0 and count_index % GROUP == 0:
            m_ext, l_ext = extend_all([(crop(m_ext, m_off, 0, own), halo), (crop(l_ext, l_off, 0, own), halo - 4)])
            m_off, l_off = halo, halo - 4
        new_off = m_off - 4
        adjoint = (
            2.0 * crop(m_ext, m_off, new_off, own)
            - crop(l_ext, l_off, new_off, own)
            + lap_valid(crop(c_ext, halo, m_off, own) * m_ext)
        )
        shape_now = adjoint.shape
        first_row = (halo - new_off) * size_y
        pick_now = rec_pick[first_row : first_row + shape_now[0] * size_y]
        injected = exact_dot(pick_now, rec_z * misfit_ext[step_index][:, None])
        adjoint = adjoint + injected.reshape(shape_now)
        gradient_field = gradient_field + crop(adjoint, new_off, 0, own) * snapshots[step_index]
        l_ext, l_off = m_ext, m_off
        m_ext, m_off = adjoint, new_off
    adjoint_first = crop(m_ext, m_off, 0, own)

    partial_blocks = to_blocks(GRADIENT_GAIN * gradient_field).reshape(slot_count, block_rows, BZ)
    pair_count = devices_all * cap_rows
    slot_for = jnp.zeros((pair_count,), jnp.int32).at[flat_slot].set(jnp.arange(slot_count, dtype=jnp.int32))
    has = jnp.zeros((pair_count,), jnp.bool_).at[flat_slot].set(True)
    parcel = jnp.where(has[:, None, None], partial_blocks[slot_for], jnp.zeros((), jnp.float32))
    parcel = parcel.reshape(devices_all, cap_rows, block_rows, BZ)
    returned = lax.all_to_all(parcel, ("shot", "blk"), split_axis=0, concat_axis=0, tiled=True)
    owned_count = model_blocks.shape[0]
    chooser = jnp.logical_and(
        lookup.reshape(-1)[None, :] == jnp.arange(owned_count, dtype=lookup.dtype)[:, None],
        filled.reshape(-1)[None, :],
    ).astype(jnp.float32)
    gradient = exact_dot(chooser, returned.reshape(pair_count, -1)).reshape(model_blocks.shape)
    return (gradient, field_end[None], adjoint_first[None])


def solution(mesh):
    in_specs = (
        P(("shot", "blk"), None, None, None),
        P(("shot", "blk")),
        P(),
        P(),
        P("shot"),
        P("shot", None),
        P("shot", "blk", None),
        P("shot", "blk", None, None),
        P("shot", "blk", None, None),
        P("shot", "blk", None, None),
        P("shot", "blk", None, None),
        P("shot", "blk", None, None),
    )
    out_specs = (
        P(("shot", "blk"), None, None, None),
        P("shot", "blk", None, None),
        P("shot", "blk", None, None),
    )
    return jax.shard_map(local, mesh=mesh, in_specs=in_specs, out_specs=out_specs, check_vma=False)
```

```python
import jax
import jax.numpy as jnp
from jax import lax
from jax.sharding import PartitionSpec as P

BX = 2
BY = 4
BZ = 128
KX = 16
KY = 8
STEPS = 8
GROUP = 4


COEFFS = (-205.0 / 72.0, 8.0 / 5.0, -1.0 / 5.0, 8.0 / 315.0, -1.0 / 560.0)
GRADIENT_GAIN = 0.0625


def from_left(x):
    count = lax.axis_size("blk")
    return lax.ppermute(x, "blk", [(i, i + 1) for i in range(count - 1)])


def from_right(x):
    count = lax.axis_size("blk")
    return lax.ppermute(x, "blk", [(i + 1, i) for i in range(count - 1)])


def pack(parts):
    return jnp.concatenate([part.reshape(-1, part.shape[-1]) for part in parts], axis=0)


def unpack(buffer, likes):
    pieces, start = [], 0
    for like in likes:
        rows = like.size // like.shape[-1]
        pieces.append(buffer[start : start + rows].reshape(like.shape))
        start += rows
    return pieces


def swap(to_right, to_left):
    got_left = unpack(from_left(pack(to_right)), to_right)
    got_right = unpack(from_right(pack(to_left)), to_left)
    return got_left, got_right


def extend_all(fields):
    tails = [cells[cells.shape[0] - width :] for cells, width in fields]
    heads = [cells[:width] for cells, width in fields]
    got_left, got_right = swap(tails, heads)
    return [
        jnp.concatenate([left, cells, right], axis=0)
        for (cells, _), left, right in zip(fields, got_left, got_right)
    ]


def crop(cells, offset, want, own):
    start = offset - want
    return cells[start : start + own + 2 * want]


def lap_valid(cells):
    extent = (cells.shape[0] - 8, cells.shape[1], cells.shape[2])
    padded = jnp.pad(cells, ((0, 0), (4, 4), (4, 4)))
    centre = padded[4 : 4 + extent[0], 4 : 4 + extent[1], 4 : 4 + extent[2]]
    summed = 3.0 * COEFFS[0] * centre
    for offset in range(1, 5):
        beside_all = (
            padded[4 + offset : 4 + offset + extent[0], 4 : 4 + extent[1], 4 : 4 + extent[2]]
            + padded[4 - offset : 4 - offset + extent[0], 4 : 4 + extent[1], 4 : 4 + extent[2]]
            + padded[4 : 4 + extent[0], 4 + offset : 4 + offset + extent[1], 4 : 4 + extent[2]]
            + padded[4 : 4 + extent[0], 4 - offset : 4 - offset + extent[1], 4 : 4 + extent[2]]
            + padded[4 : 4 + extent[0], 4 : 4 + extent[1], 4 + offset : 4 + offset + extent[2]]
            + padded[4 : 4 + extent[0], 4 : 4 + extent[1], 4 - offset : 4 - offset + extent[2]]
        )
        summed = summed + COEFFS[offset] * beside_all
    return summed


def to_piece(blocks):
    return blocks.reshape(KX, KY, BX, BY, BZ).transpose(0, 2, 1, 3, 4).reshape(KX * BX, KY * BY, BZ)


def to_blocks(field_piece):
    return (
        field_piece.reshape(KX, BX, KY, BY, BZ)
        .transpose(0, 2, 1, 3, 4)
        .reshape(KX * KY, BX, BY, BZ)
    )


def one_hot_rows(index, count):
    return (index[:, None] == jnp.arange(count, dtype=index.dtype)[None, :]).astype(jnp.float32)


def exact_dot(left, right):
    return jnp.dot(left, right, precision=lax.Precision.HIGHEST, preferred_element_type=jnp.float32)


def local(
    model_blocks,
    block_scales,
    aperture_owner,
    aperture_local,
    source_cell,
    wavelet,
    receiver_cell,
    observed,
    field_now,
    field_change,
    adjoint_last,
    adjoint_change,
):
    devices_all = lax.axis_size(("shot", "blk"))
    my_index = lax.axis_index(("shot", "blk"))
    blk_index = lax.axis_index("blk")
    slot_count = aperture_local.shape[0] // devices_all
    cap_rows = 2
    halo = 4 * GROUP

    current = field_now[0]
    before = current - field_change[0]
    own, size_y, size_z = current.shape
    plane = size_y * size_z
    adjoint_next = adjoint_last[0]
    latest = adjoint_next - adjoint_change[0]
    listen = receiver_cell[0, 0]
    listen_row = listen.astype(jnp.float32)[None, :]
    first_fields = [(current, halo), (before, halo - 4), (adjoint_next, halo), (latest, halo - 4)]
    tails = [cells[own - width :] for cells, width in first_fields] + [listen_row]
    heads = [cells[:width] for cells, width in first_fields] + [listen_row]
    got_left, got_right = swap(tails, heads)
    u_ext, b_ext, m_ext, l_ext = [
        jnp.concatenate([left, cells, right], axis=0)
        for (cells, _), left, right in zip(first_fields, got_left, got_right)
    ]
    listen_left = got_left[-1][0].astype(jnp.int32)
    listen_right = got_right[-1][0].astype(jnp.int32)

    owner_table = aperture_owner[:, 0].reshape(devices_all, slot_count)
    local_table = aperture_local.reshape(devices_all, slot_count)
    picked = owner_table == my_index
    count = jnp.sum(picked.astype(jnp.int32), axis=1)
    first = jnp.argmax(picked, axis=1)
    last = slot_count - 1 - jnp.argmax(picked[:, ::-1], axis=1)
    slot_iota = jnp.arange(slot_count, dtype=first.dtype)[None, :]
    lookup = jnp.stack(
        [
            jnp.sum(jnp.where(slot_iota == first[:, None], local_table, 0), axis=1),
            jnp.sum(jnp.where(slot_iota == last[:, None], local_table, 0), axis=1),
        ],
        axis=1,
    )
    filled = jnp.stack([count >= 1, count >= 2], axis=1)
    block_shape = model_blocks.shape[1:]
    block_rows = BX * BY
    owned_count = model_blocks.shape[0]
    pair_count = devices_all * cap_rows
    chooser = jnp.logical_and(
        lookup.reshape(-1)[:, None] == jnp.arange(owned_count, dtype=lookup.dtype)[None, :],
        filled.reshape(-1)[:, None],
    )
    table = jnp.concatenate(
        [
            model_blocks.reshape(owned_count, block_rows * BZ),
            jnp.broadcast_to(block_scales[:, None], (owned_count, BZ)),
        ],
        axis=1,
    )
    payload = jnp.dot(chooser.astype(table.dtype), table, preferred_element_type=jnp.float32)
    payload = payload.astype(model_blocks.dtype).reshape(devices_all, cap_rows, block_rows + 1, BZ)
    arrived = lax.all_to_all(payload, ("shot", "blk"), split_axis=0, concat_axis=0, tiled=True)

    my_owners = lax.dynamic_index_in_dim(owner_table, my_index, 0, keepdims=False)
    earlier = jnp.arange(slot_count)[None, :] < jnp.arange(slot_count)[:, None]
    my_ranks = jnp.sum(
        jnp.logical_and(my_owners[:, None] == my_owners[None, :], earlier).astype(jnp.int32), axis=1
    )
    flat_slot = my_owners * cap_rows + my_ranks
    slot_pick = flat_slot[:, None] == jnp.arange(pair_count, dtype=flat_slot.dtype)[None, :]
    rows = jnp.dot(
        slot_pick.astype(arrived.dtype), arrived.reshape(pair_count, (block_rows + 1) * BZ),
        preferred_element_type=jnp.float32,
    ).reshape(slot_count, block_rows + 1, BZ)
    values = rows[:, :block_rows].reshape((slot_count,) + block_shape)
    gain_rows = rows[:, block_rows, 0]
    scaled = values * gain_rows[:, None, None, None]
    courant = to_piece(scaled * scaled)
    (c_ext,) = extend_all([(courant, halo)])

    source_x = source_cell[0] // plane - blk_index * own
    source_rest = source_cell[0] % plane
    source_y = source_rest // size_z
    source_z = source_rest % size_z
    record = observed[0, 0]
    own_pick = one_hot_rows(listen // size_z, own * size_y)
    own_z = one_hot_rows(listen % size_z, size_z)

    snapshots = []
    misfit = []
    u_off, b_off = halo, halo - 4
    for step_index in range(STEPS):
        if step_index > 0 and step_index % GROUP == 0:
            u_ext, b_ext = extend_all([(crop(u_ext, u_off, 0, own), halo), (crop(b_ext, b_off, 0, own), halo - 4)])
            u_off, b_off = halo, halo - 4
        new_off = u_off - 4
        curved = lap_valid(u_ext)
        snapshots.append(crop(curved, new_off, 0, own))
        advanced = (
            2.0 * crop(u_ext, u_off, new_off, own)
            - crop(b_ext, b_off, new_off, own)
            + crop(c_ext, halo, new_off, own) * curved
        )
        shape_now = advanced.shape
        at_source = (
            (lax.broadcasted_iota(jnp.int32, shape_now, 0) == source_x + new_off)
            & (lax.broadcasted_iota(jnp.int32, shape_now, 1) == source_y)
            & (lax.broadcasted_iota(jnp.int32, shape_now, 2) == source_z)
        )
        advanced = advanced + jnp.where(at_source, wavelet[0, step_index], jnp.zeros((), jnp.float32))
        sampled = exact_dot(own_pick, crop(advanced, new_off, 0, own).reshape(own * size_y, size_z))
        misfit.append(jnp.sum(sampled * own_z, axis=1) - record[step_index])
        b_ext, b_off = u_ext, u_off
        u_ext, u_off = advanced, new_off
    field_end = crop(u_ext, u_off, 0, own)

    misfit_all = jnp.stack(misfit)
    (misfit_left,), (misfit_right,) = swap([misfit_all], [misfit_all])
    misfit_ext = jnp.concatenate([misfit_left, misfit_all, misfit_right], axis=1)
    cells_all = jnp.concatenate([listen_left, listen, listen_right])
    shift_all = jnp.concatenate(
        [
            jnp.full(listen.shape, -own, jnp.int32),
            jnp.zeros(listen.shape, jnp.int32),
            jnp.full(listen.shape, own, jnp.int32),
        ]
    )
    rec_x = cells_all // plane + shift_all + halo
    rec_plane = jnp.where(
        jnp.logical_and(rec_x >= 0, rec_x < own + 2 * halo), rec_x * size_y + (cells_all % plane) // size_z, -1
    )
    rec_pick = (
        jnp.arange((own + 2 * halo) * size_y, dtype=jnp.int32)[:, None] == rec_plane[None, :]
    ).astype(jnp.float32)
    rec_z = one_hot_rows(cells_all % size_z, size_z)

    m_off, l_off = halo, halo - 4
    gradient_field = jnp.zeros_like(adjoint_next)
    for count_index, step_index in enumerate(range(STEPS - 1, -1, -1)):
        if count_index > 0 and count_index % GROUP == 0:
            m_ext, l_ext = extend_all([(crop(m_ext, m_off, 0, own), halo), (crop(l_ext, l_off, 0, own), halo - 4)])
            m_off, l_off = halo, halo - 4
        new_off = m_off - 4
        adjoint = (
            2.0 * crop(m_ext, m_off, new_off, own)
            - crop(l_ext, l_off, new_off, own)
            + lap_valid(crop(c_ext, halo, m_off, own) * m_ext)
        )
        shape_now = adjoint.shape
        first_row = (halo - new_off) * size_y
        pick_now = rec_pick[first_row : first_row + shape_now[0] * size_y]
        injected = exact_dot(pick_now, rec_z * misfit_ext[step_index][:, None])
        adjoint = adjoint + injected.reshape(shape_now)
        gradient_field = gradient_field + crop(adjoint, new_off, 0, own) * snapshots[step_index]
        l_ext, l_off = m_ext, m_off
        m_ext, m_off = adjoint, new_off
    adjoint_first = crop(m_ext, m_off, 0, own)

    partial_blocks = to_blocks(GRADIENT_GAIN * gradient_field).reshape(slot_count, block_rows, BZ)
    parcel = exact_dot(slot_pick.T.astype(jnp.float32), partial_blocks.reshape(slot_count, block_rows * BZ))
    parcel = parcel.reshape(devices_all, cap_rows, block_rows, BZ)
    returned = lax.all_to_all(parcel, ("shot", "blk"), split_axis=0, concat_axis=0, tiled=True)
    gradient = exact_dot(chooser.T.astype(jnp.float32), returned.reshape(pair_count, -1)).reshape(model_blocks.shape)
    return (gradient, field_end[None], adjoint_first[None])


def solution(mesh):
    in_specs = (
        P(("shot", "blk"), None, None, None),
        P(("shot", "blk")),
        P(),
        P(),
        P("shot"),
        P("shot", None),
        P("shot", "blk", None),
        P("shot", "blk", None, None),
        P("shot", "blk", None, None),
        P("shot", "blk", None, None),
        P("shot", "blk", None, None),
        P("shot", "blk", None, None),
    )
    out_specs = (
        P(("shot", "blk"), None, None, None),
        P("shot", "blk", None, None),
        P("shot", "blk", None, None),
    )
    return jax.shard_map(local, mesh=mesh, in_specs=in_specs, out_specs=out_specs, check_vma=False)
```

```python
import jax
import jax.numpy as jnp
from jax import lax
from jax.sharding import PartitionSpec as P


BX = 2
BY = 4
BZ = 128
KX = 16
KY = 8
STEPS = 8
GROUP = 4


COEFFS = (-205.0 / 72.0, 8.0 / 5.0, -1.0 / 5.0, 8.0 / 315.0, -1.0 / 560.0)
GRADIENT_GAIN = 0.0625


def from_left(x):
    count = lax.axis_size("blk")
    return lax.ppermute(x, "blk", [(i, i + 1) for i in range(count - 1)])


def from_right(x):
    count = lax.axis_size("blk")
    return lax.ppermute(x, "blk", [(i + 1, i) for i in range(count - 1)])


def pack(parts):
    return jnp.concatenate([part.reshape(-1, part.shape[-1]) for part in parts], axis=0)


def unpack(buffer, likes):
    pieces, start = [], 0
    for like in likes:
        rows = like.size // like.shape[-1]
        pieces.append(buffer[start : start + rows].reshape(like.shape))
        start += rows
    return pieces


def swap(to_right, to_left):
    got_left = unpack(from_left(pack(to_right)), to_right)
    got_right = unpack(from_right(pack(to_left)), to_left)
    return got_left, got_right


def extend_all(fields):
    tails = [cells[cells.shape[0] - width :] for cells, width in fields]
    heads = [cells[:width] for cells, width in fields]
    got_left, got_right = swap(tails, heads)
    return [
        jnp.concatenate([left, cells, right], axis=0)
        for (cells, _), left, right in zip(fields, got_left, got_right)
    ]


def crop(cells, offset, want, own):
    start = offset - want
    return cells[start : start + own + 2 * want]


def lap_valid(cells):
    extent = (cells.shape[0] - 8, cells.shape[1], cells.shape[2])
    padded = jnp.pad(cells, ((0, 0), (4, 4), (4, 4)))
    centre = padded[4 : 4 + extent[0], 4 : 4 + extent[1], 4 : 4 + extent[2]]
    summed = 3.0 * COEFFS[0] * centre
    for offset in range(1, 5):
        beside_all = (
            padded[4 + offset : 4 + offset + extent[0], 4 : 4 + extent[1], 4 : 4 + extent[2]]
            + padded[4 - offset : 4 - offset + extent[0], 4 : 4 + extent[1], 4 : 4 + extent[2]]
            + padded[4 : 4 + extent[0], 4 + offset : 4 + offset + extent[1], 4 : 4 + extent[2]]
            + padded[4 : 4 + extent[0], 4 - offset : 4 - offset + extent[1], 4 : 4 + extent[2]]
            + padded[4 : 4 + extent[0], 4 : 4 + extent[1], 4 + offset : 4 + offset + extent[2]]
            + padded[4 : 4 + extent[0], 4 : 4 + extent[1], 4 - offset : 4 - offset + extent[2]]
        )
        summed = summed + COEFFS[offset] * beside_all
    return summed


def to_piece(blocks):
    return blocks.reshape(KX, KY, BX, BY, BZ).transpose(0, 2, 1, 3, 4).reshape(KX * BX, KY * BY, BZ)


def to_blocks(field_piece):
    return (
        field_piece.reshape(KX, BX, KY, BY, BZ)
        .transpose(0, 2, 1, 3, 4)
        .reshape(KX * KY, BX, BY, BZ)
    )


def one_hot_rows(index, count):
    return (index[:, None] == jnp.arange(count, dtype=index.dtype)[None, :]).astype(jnp.float32)


def exact_dot(left, right):
    return jnp.dot(left, right, precision=lax.Precision.HIGHEST, preferred_element_type=jnp.float32)


def local(
    model_blocks,
    block_scales,
    aperture_owner,
    aperture_local,
    source_cell,
    wavelet,
    receiver_cell,
    observed,
    field_now,
    field_change,
    adjoint_last,
    adjoint_change,
):
    devices_all = lax.axis_size(("shot", "blk"))
    my_index = lax.axis_index(("shot", "blk"))
    blk_index = lax.axis_index("blk")
    slot_count = aperture_local.shape[0] // devices_all
    cap_rows = 2
    halo = 4 * GROUP

    own, size_y, size_z = field_now.shape[1:]
    plane = size_y * size_z
    listen = receiver_cell[0, 0]
    current = field_now[0]
    before = current - field_change[0]
    adjoint_next = adjoint_last[0]
    latest = adjoint_next - adjoint_change[0]
    listen_row = listen.astype(jnp.float32)[None, :]
    first_fields = [(current, halo), (before, halo - 4), (adjoint_next, halo), (latest, halo - 4)]
    tails = [cells[own - width :] for cells, width in first_fields] + [listen_row]
    heads = [cells[:width] for cells, width in first_fields] + [listen_row]
    to_right, to_left = pack(tails), pack(heads)
    got_left = unpack(from_left(to_right), tails)
    got_right = unpack(from_right(to_left), heads)
    u_ext, b_ext, m_ext, l_ext = [
        jnp.concatenate([left, cells, right], axis=0)
        for (cells, _), left, right in zip(first_fields, got_left, got_right)
    ]
    listen_left = got_left[-1][0].astype(jnp.int32)
    listen_right = got_right[-1][0].astype(jnp.int32)

    owner_table = aperture_owner[:, 0].reshape(devices_all, slot_count)
    local_table = aperture_local.reshape(devices_all, slot_count)
    picked = owner_table == my_index
    count = jnp.sum(picked.astype(jnp.int32), axis=1)
    first = jnp.argmax(picked, axis=1)
    last = slot_count - 1 - jnp.argmax(picked[:, ::-1], axis=1)
    slot_iota = jnp.arange(slot_count, dtype=first.dtype)[None, :]
    lookup = jnp.stack(
        [
            jnp.sum(jnp.where(slot_iota == first[:, None], local_table, 0), axis=1),
            jnp.sum(jnp.where(slot_iota == last[:, None], local_table, 0), axis=1),
        ],
        axis=1,
    )
    filled = jnp.stack([count >= 1, count >= 2], axis=1)
    block_shape = model_blocks.shape[1:]
    block_rows = BX * BY
    owned_count = model_blocks.shape[0]
    pair_count = devices_all * cap_rows
    chooser = jnp.logical_and(
        lookup.reshape(-1)[:, None] == jnp.arange(owned_count, dtype=lookup.dtype)[None, :],
        filled.reshape(-1)[:, None],
    )
    table = jnp.concatenate(
        [
            model_blocks.reshape(owned_count, block_rows * BZ),
            jnp.broadcast_to(block_scales[:, None], (owned_count, BZ)),
        ],
        axis=1,
    )
    payload = jnp.dot(chooser.astype(table.dtype), table, preferred_element_type=jnp.float32)
    payload = payload.astype(model_blocks.dtype).reshape(devices_all, cap_rows, block_rows + 1, BZ)
    arrived = lax.all_to_all(payload, ("shot", "blk"), split_axis=0, concat_axis=0, tiled=True)

    my_owners = lax.dynamic_index_in_dim(owner_table, my_index, 0, keepdims=False)
    earlier = jnp.arange(slot_count)[None, :] < jnp.arange(slot_count)[:, None]
    my_ranks = jnp.sum(
        jnp.logical_and(my_owners[:, None] == my_owners[None, :], earlier).astype(jnp.int32), axis=1
    )
    flat_slot = my_owners * cap_rows + my_ranks
    slot_pick = flat_slot[:, None] == jnp.arange(pair_count, dtype=flat_slot.dtype)[None, :]
    rows = jnp.dot(
        slot_pick.astype(arrived.dtype), arrived.reshape(pair_count, (block_rows + 1) * BZ),
        preferred_element_type=jnp.float32,
    ).reshape(slot_count, block_rows + 1, BZ)
    values = rows[:, :block_rows].reshape((slot_count,) + block_shape)
    gain_rows = rows[:, block_rows, 0]
    scaled = values * gain_rows[:, None, None, None]
    courant = to_piece(scaled * scaled)
    (c_ext,) = extend_all([(courant, halo)])

    source_x = source_cell[0] // plane - blk_index * own
    source_rest = source_cell[0] % plane
    source_y = source_rest // size_z
    source_z = source_rest % size_z
    record = observed[0, 0]
    own_pick = one_hot_rows(listen // size_z, own * size_y)
    own_z = one_hot_rows(listen % size_z, size_z)

    snapshots = []
    misfit = []
    u_off, b_off = halo, halo - 4
    for step_index in range(STEPS):
        if step_index > 0 and step_index % GROUP == 0:
            u_ext, b_ext = extend_all([(crop(u_ext, u_off, 0, own), halo), (crop(b_ext, b_off, 0, own), halo - 4)])
            u_off, b_off = halo, halo - 4
        new_off = u_off - 4
        curved = lap_valid(u_ext)
        snapshots.append(crop(curved, new_off, 0, own))
        advanced = (
            2.0 * crop(u_ext, u_off, new_off, own)
            - crop(b_ext, b_off, new_off, own)
            + crop(c_ext, halo, new_off, own) * curved
        )
        shape_now = advanced.shape
        at_source = (
            (lax.broadcasted_iota(jnp.int32, shape_now, 0) == source_x + new_off)
            & (lax.broadcasted_iota(jnp.int32, shape_now, 1) == source_y)
            & (lax.broadcasted_iota(jnp.int32, shape_now, 2) == source_z)
        )
        advanced = advanced + jnp.where(at_source, wavelet[0, step_index], jnp.zeros((), jnp.float32))
        sampled = exact_dot(own_pick, crop(advanced, new_off, 0, own).reshape(own * size_y, size_z))
        misfit.append(jnp.sum(sampled * own_z, axis=1) - record[step_index])
        b_ext, b_off = u_ext, u_off
        u_ext, u_off = advanced, new_off
    field_end = crop(u_ext, u_off, 0, own)

    misfit_all = jnp.stack(misfit)
    (misfit_left,), (misfit_right,) = swap([misfit_all], [misfit_all])
    misfit_ext = jnp.concatenate([misfit_left, misfit_all, misfit_right], axis=1)
    cells_all = jnp.concatenate([listen_left, listen, listen_right])
    shift_all = jnp.concatenate(
        [
            jnp.full(listen.shape, -own, jnp.int32),
            jnp.zeros(listen.shape, jnp.int32),
            jnp.full(listen.shape, own, jnp.int32),
        ]
    )
    rec_x = cells_all // plane + shift_all + halo
    rec_plane = jnp.where(
        jnp.logical_and(rec_x >= 0, rec_x < own + 2 * halo), rec_x * size_y + (cells_all % plane) // size_z, -1
    )
    rec_pick = (
        jnp.arange((own + 2 * halo) * size_y, dtype=jnp.int32)[:, None] == rec_plane[None, :]
    ).astype(jnp.float32)
    rec_z = one_hot_rows(cells_all % size_z, size_z)

    m_off, l_off = halo, halo - 4
    gradient_field = jnp.zeros_like(adjoint_next)
    for count_index, step_index in enumerate(range(STEPS - 1, -1, -1)):
        if count_index > 0 and count_index % GROUP == 0:
            m_ext, l_ext = extend_all([(crop(m_ext, m_off, 0, own), halo), (crop(l_ext, l_off, 0, own), halo - 4)])
            m_off, l_off = halo, halo - 4
        new_off = m_off - 4
        adjoint = (
            2.0 * crop(m_ext, m_off, new_off, own)
            - crop(l_ext, l_off, new_off, own)
            + lap_valid(crop(c_ext, halo, m_off, own) * m_ext)
        )
        shape_now = adjoint.shape
        first_row = (halo - new_off) * size_y
        pick_now = rec_pick[first_row : first_row + shape_now[0] * size_y]
        injected = exact_dot(pick_now, rec_z * misfit_ext[step_index][:, None])
        adjoint = adjoint + injected.reshape(shape_now)
        gradient_field = gradient_field + crop(adjoint, new_off, 0, own) * snapshots[step_index]
        l_ext, l_off = m_ext, m_off
        m_ext, m_off = adjoint, new_off
    adjoint_first = crop(m_ext, m_off, 0, own)

    partial_blocks = to_blocks(GRADIENT_GAIN * gradient_field).reshape(slot_count, block_rows, BZ)
    parcel = exact_dot(slot_pick.T.astype(jnp.float32), partial_blocks.reshape(slot_count, block_rows * BZ))
    parcel = parcel.reshape(devices_all, cap_rows, block_rows, BZ)
    returned = lax.all_to_all(parcel, ("shot", "blk"), split_axis=0, concat_axis=0, tiled=True)
    gradient = exact_dot(chooser.T.astype(jnp.float32), returned.reshape(pair_count, -1)).reshape(model_blocks.shape)
    return (gradient, field_end[None], adjoint_first[None])


def solution(mesh):
    in_specs = (
        P(("shot", "blk"), None, None, None),
        P(("shot", "blk")),
        P(),
        P(),
        P("shot"),
        P("shot", None),
        P("shot", "blk", None),
        P("shot", "blk", None, None),
        P("shot", "blk", None, None),
        P("shot", "blk", None, None),
        P("shot", "blk", None, None),
        P("shot", "blk", None, None),
    )
    out_specs = (
        P(("shot", "blk"), None, None, None),
        P("shot", "blk", None, None),
        P("shot", "blk", None, None),
    )

    return jax.shard_map(local, mesh=mesh, in_specs=in_specs, out_specs=out_specs, check_vma=False)
```

```python
import jax
import jax.numpy as jnp
from jax import lax
from jax.sharding import PartitionSpec as P


BX = 2
BY = 4
BZ = 128
KX = 16
KY = 8
STEPS = 8
GROUP = 4


COEFFS = (-205.0 / 72.0, 8.0 / 5.0, -1.0 / 5.0, 8.0 / 315.0, -1.0 / 560.0)
GRADIENT_GAIN = 0.0625


def from_left(x):
    count = lax.axis_size("blk")
    return lax.ppermute(x, "blk", [(i, i + 1) for i in range(count - 1)])


def from_right(x):
    count = lax.axis_size("blk")
    return lax.ppermute(x, "blk", [(i + 1, i) for i in range(count - 1)])


def pack(parts):
    return jnp.concatenate([part.reshape(-1, part.shape[-1]) for part in parts], axis=0)


def unpack(buffer, likes):
    pieces, start = [], 0
    for like in likes:
        rows = like.size // like.shape[-1]
        pieces.append(buffer[start : start + rows].reshape(like.shape))
        start += rows
    return pieces


def swap(to_right, to_left):
    got_left = unpack(from_left(pack(to_right)), to_right)
    got_right = unpack(from_right(pack(to_left)), to_left)
    return got_left, got_right


def extend_all(fields):
    tails = [cells[cells.shape[0] - width :] for cells, width in fields]
    heads = [cells[:width] for cells, width in fields]
    got_left, got_right = swap(tails, heads)
    return [
        jnp.concatenate([left, cells, right], axis=0)
        for (cells, _), left, right in zip(fields, got_left, got_right)
    ]


def crop(cells, offset, want, own):
    start = offset - want
    return cells[start : start + own + 2 * want]


def lap_valid(cells):
    extent = (cells.shape[0] - 8, cells.shape[1], cells.shape[2])
    padded = jnp.pad(cells, ((0, 0), (4, 4), (4, 4)))
    centre = padded[4 : 4 + extent[0], 4 : 4 + extent[1], 4 : 4 + extent[2]]
    summed = 3.0 * COEFFS[0] * centre
    for offset in range(1, 5):
        beside_all = (
            padded[4 + offset : 4 + offset + extent[0], 4 : 4 + extent[1], 4 : 4 + extent[2]]
            + padded[4 - offset : 4 - offset + extent[0], 4 : 4 + extent[1], 4 : 4 + extent[2]]
            + padded[4 : 4 + extent[0], 4 + offset : 4 + offset + extent[1], 4 : 4 + extent[2]]
            + padded[4 : 4 + extent[0], 4 - offset : 4 - offset + extent[1], 4 : 4 + extent[2]]
            + padded[4 : 4 + extent[0], 4 : 4 + extent[1], 4 + offset : 4 + offset + extent[2]]
            + padded[4 : 4 + extent[0], 4 : 4 + extent[1], 4 - offset : 4 - offset + extent[2]]
        )
        summed = summed + COEFFS[offset] * beside_all
    return summed


def to_piece(blocks):
    return blocks.reshape(KX, KY, BX, BY, BZ).transpose(0, 2, 1, 3, 4).reshape(KX * BX, KY * BY, BZ)


def to_blocks(field_piece):
    return (
        field_piece.reshape(KX, BX, KY, BY, BZ)
        .transpose(0, 2, 1, 3, 4)
        .reshape(KX * KY, BX, BY, BZ)
    )


def one_hot_rows(index, count):
    return (index[:, None] == jnp.arange(count, dtype=index.dtype)[None, :]).astype(jnp.float32)


def exact_dot(left, right):
    return jnp.dot(left, right, precision=lax.Precision.HIGHEST, preferred_element_type=jnp.float32)


def local(
    model_blocks,
    block_scales,
    aperture_owner,
    aperture_local,
    source_cell,
    wavelet,
    receiver_cell,
    observed,
    field_now,
    field_change,
    adjoint_last,
    adjoint_change,
):
    devices_all = lax.axis_size(("shot", "blk"))
    my_index = lax.axis_index(("shot", "blk"))
    blk_index = lax.axis_index("blk")
    slot_count = aperture_local.shape[0] // devices_all
    cap_rows = 2
    halo = 4 * GROUP

    own, size_y, size_z = field_now.shape[1:]
    plane = size_y * size_z
    listen = receiver_cell[0, 0]
    current = field_now[0]
    before = current - field_change[0]
    listen_row = listen.astype(jnp.float32)[None, :]
    first_fields = [(current, halo), (before, halo - 4)]
    tails = [cells[own - width :] for cells, width in first_fields] + [listen_row]
    heads = [cells[:width] for cells, width in first_fields] + [listen_row]
    to_right, to_left = pack(tails), pack(heads)
    got_left = unpack(from_left(to_right), tails)
    got_right = unpack(from_right(to_left), heads)
    u_ext, b_ext = [
        jnp.concatenate([left, cells, right], axis=0)
        for (cells, _), left, right in zip(first_fields, got_left, got_right)
    ]
    adjoint_next = adjoint_last[0]
    latest = adjoint_next - adjoint_change[0]
    adjoint_fields = [(adjoint_next, halo), (latest, halo - 4)]
    adjoint_tails = [cells[own - width :] for cells, width in adjoint_fields]
    adjoint_heads = [cells[:width] for cells, width in adjoint_fields]
    adjoint_from_left = from_left(pack(adjoint_tails))
    adjoint_from_right = from_right(pack(adjoint_heads))
    listen_left = got_left[-1][0].astype(jnp.int32)
    listen_right = got_right[-1][0].astype(jnp.int32)

    owner_table = aperture_owner[:, 0].reshape(devices_all, slot_count)
    local_table = aperture_local.reshape(devices_all, slot_count)
    picked = owner_table == my_index
    count = jnp.sum(picked.astype(jnp.int32), axis=1)
    first = jnp.argmax(picked, axis=1)
    last = slot_count - 1 - jnp.argmax(picked[:, ::-1], axis=1)
    slot_iota = jnp.arange(slot_count, dtype=first.dtype)[None, :]
    lookup = jnp.stack(
        [
            jnp.sum(jnp.where(slot_iota == first[:, None], local_table, 0), axis=1),
            jnp.sum(jnp.where(slot_iota == last[:, None], local_table, 0), axis=1),
        ],
        axis=1,
    )
    filled = jnp.stack([count >= 1, count >= 2], axis=1)
    block_shape = model_blocks.shape[1:]
    block_rows = BX * BY
    owned_count = model_blocks.shape[0]
    pair_count = devices_all * cap_rows
    chooser = jnp.logical_and(
        lookup.reshape(-1)[:, None] == jnp.arange(owned_count, dtype=lookup.dtype)[None, :],
        filled.reshape(-1)[:, None],
    )
    table = jnp.concatenate(
        [
            model_blocks.reshape(owned_count, block_rows * BZ),
            jnp.broadcast_to(block_scales[:, None], (owned_count, BZ)),
        ],
        axis=1,
    )
    payload = jnp.dot(chooser.astype(table.dtype), table, preferred_element_type=jnp.float32)
    payload = payload.astype(model_blocks.dtype).reshape(devices_all, cap_rows, block_rows + 1, BZ)
    arrived = lax.all_to_all(payload, ("shot", "blk"), split_axis=0, concat_axis=0, tiled=True)

    my_owners = lax.dynamic_index_in_dim(owner_table, my_index, 0, keepdims=False)
    earlier = jnp.arange(slot_count)[None, :] < jnp.arange(slot_count)[:, None]
    my_ranks = jnp.sum(
        jnp.logical_and(my_owners[:, None] == my_owners[None, :], earlier).astype(jnp.int32), axis=1
    )
    flat_slot = my_owners * cap_rows + my_ranks
    slot_pick = flat_slot[:, None] == jnp.arange(pair_count, dtype=flat_slot.dtype)[None, :]
    rows = jnp.dot(
        slot_pick.astype(arrived.dtype), arrived.reshape(pair_count, (block_rows + 1) * BZ),
        preferred_element_type=jnp.float32,
    ).reshape(slot_count, block_rows + 1, BZ)
    values = rows[:, :block_rows].reshape((slot_count,) + block_shape)
    gain_rows = rows[:, block_rows, 0]
    scaled = values * gain_rows[:, None, None, None]
    courant = to_piece(scaled * scaled)
    (c_ext,) = extend_all([(courant, halo)])

    source_x = source_cell[0] // plane - blk_index * own
    source_rest = source_cell[0] % plane
    source_y = source_rest // size_z
    source_z = source_rest % size_z
    record = observed[0, 0]
    own_pick = one_hot_rows(listen // size_z, own * size_y)
    own_z = one_hot_rows(listen % size_z, size_z)

    snapshots = []
    misfit = []
    u_off, b_off = halo, halo - 4
    for step_index in range(STEPS):
        if step_index > 0 and step_index % GROUP == 0:
            u_ext, b_ext = extend_all([(crop(u_ext, u_off, 0, own), halo), (crop(b_ext, b_off, 0, own), halo - 4)])
            u_off, b_off = halo, halo - 4
        new_off = u_off - 4
        curved = lap_valid(u_ext)
        snapshots.append(crop(curved, new_off, 0, own))
        advanced = (
            2.0 * crop(u_ext, u_off, new_off, own)
            - crop(b_ext, b_off, new_off, own)
            + crop(c_ext, halo, new_off, own) * curved
        )
        shape_now = advanced.shape
        at_source = (
            (lax.broadcasted_iota(jnp.int32, shape_now, 0) == source_x + new_off)
            & (lax.broadcasted_iota(jnp.int32, shape_now, 1) == source_y)
            & (lax.broadcasted_iota(jnp.int32, shape_now, 2) == source_z)
        )
        advanced = advanced + jnp.where(at_source, wavelet[0, step_index], jnp.zeros((), jnp.float32))
        sampled = exact_dot(own_pick, crop(advanced, new_off, 0, own).reshape(own * size_y, size_z))
        misfit.append(jnp.sum(sampled * own_z, axis=1) - record[step_index])
        b_ext, b_off = u_ext, u_off
        u_ext, u_off = advanced, new_off
    field_end = crop(u_ext, u_off, 0, own)

    misfit_all = jnp.stack(misfit)
    misfit_all, adjoint_from_left, adjoint_from_right = lax.optimization_barrier(
        (misfit_all, adjoint_from_left, adjoint_from_right)
    )
    m_ext, l_ext = [
        jnp.concatenate([left, cells, right], axis=0)
        for (cells, _), left, right in zip(
            adjoint_fields,
            unpack(adjoint_from_left, adjoint_tails),
            unpack(adjoint_from_right, adjoint_heads),
        )
    ]
    (misfit_left,), (misfit_right,) = swap([misfit_all], [misfit_all])
    misfit_ext = jnp.concatenate([misfit_left, misfit_all, misfit_right], axis=1)
    cells_all = jnp.concatenate([listen_left, listen, listen_right])
    shift_all = jnp.concatenate(
        [
            jnp.full(listen.shape, -own, jnp.int32),
            jnp.zeros(listen.shape, jnp.int32),
            jnp.full(listen.shape, own, jnp.int32),
        ]
    )
    rec_x = cells_all // plane + shift_all + halo
    rec_plane = jnp.where(
        jnp.logical_and(rec_x >= 0, rec_x < own + 2 * halo), rec_x * size_y + (cells_all % plane) // size_z, -1
    )
    rec_pick = (
        jnp.arange((own + 2 * halo) * size_y, dtype=jnp.int32)[:, None] == rec_plane[None, :]
    ).astype(jnp.float32)
    rec_z = one_hot_rows(cells_all % size_z, size_z)

    m_off, l_off = halo, halo - 4
    gradient_field = jnp.zeros_like(adjoint_next)
    for count_index, step_index in enumerate(range(STEPS - 1, -1, -1)):
        if count_index > 0 and count_index % GROUP == 0:
            m_ext, l_ext = extend_all([(crop(m_ext, m_off, 0, own), halo), (crop(l_ext, l_off, 0, own), halo - 4)])
            m_off, l_off = halo, halo - 4
        new_off = m_off - 4
        adjoint = (
            2.0 * crop(m_ext, m_off, new_off, own)
            - crop(l_ext, l_off, new_off, own)
            + lap_valid(crop(c_ext, halo, m_off, own) * m_ext)
        )
        shape_now = adjoint.shape
        first_row = (halo - new_off) * size_y
        pick_now = rec_pick[first_row : first_row + shape_now[0] * size_y]
        injected = exact_dot(pick_now, rec_z * misfit_ext[step_index][:, None])
        adjoint = adjoint + injected.reshape(shape_now)
        gradient_field = gradient_field + crop(adjoint, new_off, 0, own) * snapshots[step_index]
        l_ext, l_off = m_ext, m_off
        m_ext, m_off = adjoint, new_off
    adjoint_first = crop(m_ext, m_off, 0, own)

    partial_blocks = to_blocks(GRADIENT_GAIN * gradient_field).reshape(slot_count, block_rows, BZ)
    parcel = exact_dot(slot_pick.T.astype(jnp.float32), partial_blocks.reshape(slot_count, block_rows * BZ))
    parcel = parcel.reshape(devices_all, cap_rows, block_rows, BZ)
    returned = lax.all_to_all(parcel, ("shot", "blk"), split_axis=0, concat_axis=0, tiled=True)
    gradient = exact_dot(chooser.T.astype(jnp.float32), returned.reshape(pair_count, -1)).reshape(model_blocks.shape)
    return (gradient, field_end[None], adjoint_first[None])


def solution(mesh):
    in_specs = (
        P(("shot", "blk"), None, None, None),
        P(("shot", "blk")),
        P(),
        P(),
        P("shot"),
        P("shot", None),
        P("shot", "blk", None),
        P("shot", "blk", None, None),
        P("shot", "blk", None, None),
        P("shot", "blk", None, None),
        P("shot", "blk", None, None),
        P("shot", "blk", None, None),
    )
    out_specs = (
        P(("shot", "blk"), None, None, None),
        P("shot", "blk", None, None),
        P("shot", "blk", None, None),
    )

    return jax.shard_map(local, mesh=mesh, in_specs=in_specs, out_specs=out_specs, check_vma=False)
```

```python
import jax
import jax.numpy as jnp
from jax import lax
from jax.sharding import PartitionSpec as P


BX = 2
BY = 4
BZ = 128
KX = 16
KY = 8
STEPS = 8
GROUP = 4


COEFFS = (-205.0 / 72.0, 8.0 / 5.0, -1.0 / 5.0, 8.0 / 315.0, -1.0 / 560.0)
GRADIENT_GAIN = 0.0625


def from_left(x):
    count = lax.axis_size("blk")
    return lax.ppermute(x, "blk", [(i, i + 1) for i in range(count - 1)])


def from_right(x):
    count = lax.axis_size("blk")
    return lax.ppermute(x, "blk", [(i + 1, i) for i in range(count - 1)])


def pack(parts):
    return jnp.concatenate([part.reshape(-1, part.shape[-1]) for part in parts], axis=0)


def unpack(buffer, likes):
    pieces, start = [], 0
    for like in likes:
        rows = like.size // like.shape[-1]
        pieces.append(buffer[start : start + rows].reshape(like.shape))
        start += rows
    return pieces


def swap(to_right, to_left):
    got_left = unpack(from_left(pack(to_right)), to_right)
    got_right = unpack(from_right(pack(to_left)), to_left)
    return got_left, got_right


def extend_all(fields):
    tails = [cells[cells.shape[0] - width :] for cells, width in fields]
    heads = [cells[:width] for cells, width in fields]
    got_left, got_right = swap(tails, heads)
    return [
        jnp.concatenate([left, cells, right], axis=0)
        for (cells, _), left, right in zip(fields, got_left, got_right)
    ]


def crop(cells, offset, want, own):
    start = offset - want
    return cells[start : start + own + 2 * want]


def lap_valid(cells):
    extent = (cells.shape[0] - 8, cells.shape[1], cells.shape[2])
    padded = jnp.pad(cells, ((0, 0), (4, 4), (4, 4)))
    centre = padded[4 : 4 + extent[0], 4 : 4 + extent[1], 4 : 4 + extent[2]]
    summed = 3.0 * COEFFS[0] * centre
    for offset in range(1, 5):
        beside_all = (
            padded[4 + offset : 4 + offset + extent[0], 4 : 4 + extent[1], 4 : 4 + extent[2]]
            + padded[4 - offset : 4 - offset + extent[0], 4 : 4 + extent[1], 4 : 4 + extent[2]]
            + padded[4 : 4 + extent[0], 4 + offset : 4 + offset + extent[1], 4 : 4 + extent[2]]
            + padded[4 : 4 + extent[0], 4 - offset : 4 - offset + extent[1], 4 : 4 + extent[2]]
            + padded[4 : 4 + extent[0], 4 : 4 + extent[1], 4 + offset : 4 + offset + extent[2]]
            + padded[4 : 4 + extent[0], 4 : 4 + extent[1], 4 - offset : 4 - offset + extent[2]]
        )
        summed = summed + COEFFS[offset] * beside_all
    return summed


def to_piece(blocks):
    return blocks.reshape(KX, KY, BX, BY, BZ).transpose(0, 2, 1, 3, 4).reshape(KX * BX, KY * BY, BZ)


def to_blocks(field_piece):
    return (
        field_piece.reshape(KX, BX, KY, BY, BZ)
        .transpose(0, 2, 1, 3, 4)
        .reshape(KX * KY, BX, BY, BZ)
    )


def one_hot_rows(index, count):
    return (index[:, None] == jnp.arange(count, dtype=index.dtype)[None, :]).astype(jnp.float32)


def exact_dot(left, right):
    return jnp.dot(left, right, precision=lax.Precision.HIGHEST, preferred_element_type=jnp.float32)


def pick_dot(one_hot, values):
    return jnp.dot(one_hot, values, precision=lax.Precision.HIGH, preferred_element_type=jnp.float32)


def local(
    model_blocks,
    block_scales,
    aperture_owner,
    aperture_local,
    source_cell,
    wavelet,
    receiver_cell,
    observed,
    field_now,
    field_change,
    adjoint_last,
    adjoint_change,
):
    devices_all = lax.axis_size(("shot", "blk"))
    my_index = lax.axis_index(("shot", "blk"))
    blk_index = lax.axis_index("blk")
    slot_count = aperture_local.shape[0] // devices_all
    cap_rows = 2
    halo = 4 * GROUP

    own, size_y, size_z = field_now.shape[1:]
    plane = size_y * size_z
    listen = receiver_cell[0, 0]
    current = field_now[0]
    before = current - field_change[0]
    listen_row = listen.astype(jnp.float32)[None, :]
    first_fields = [(current, halo), (before, halo - 4)]
    tails = [cells[own - width :] for cells, width in first_fields] + [listen_row]
    heads = [cells[:width] for cells, width in first_fields] + [listen_row]
    to_right, to_left = pack(tails), pack(heads)
    got_left = unpack(from_left(to_right), tails)
    got_right = unpack(from_right(to_left), heads)
    u_ext, b_ext = [
        jnp.concatenate([left, cells, right], axis=0)
        for (cells, _), left, right in zip(first_fields, got_left, got_right)
    ]
    adjoint_next = adjoint_last[0]
    latest = adjoint_next - adjoint_change[0]
    adjoint_fields = [(adjoint_next, halo), (latest, halo - 4)]
    adjoint_tails = [cells[own - width :] for cells, width in adjoint_fields]
    adjoint_heads = [cells[:width] for cells, width in adjoint_fields]
    adjoint_from_left = from_left(pack(adjoint_tails))
    adjoint_from_right = from_right(pack(adjoint_heads))
    listen_left = got_left[-1][0].astype(jnp.int32)
    listen_right = got_right[-1][0].astype(jnp.int32)

    owner_table = aperture_owner[:, 0].reshape(devices_all, slot_count)
    local_table = aperture_local.reshape(devices_all, slot_count)
    picked = owner_table == my_index
    count = jnp.sum(picked.astype(jnp.int32), axis=1)
    first = jnp.argmax(picked, axis=1)
    last = slot_count - 1 - jnp.argmax(picked[:, ::-1], axis=1)
    slot_iota = jnp.arange(slot_count, dtype=first.dtype)[None, :]
    lookup = jnp.stack(
        [
            jnp.sum(jnp.where(slot_iota == first[:, None], local_table, 0), axis=1),
            jnp.sum(jnp.where(slot_iota == last[:, None], local_table, 0), axis=1),
        ],
        axis=1,
    )
    filled = jnp.stack([count >= 1, count >= 2], axis=1)
    block_shape = model_blocks.shape[1:]
    block_rows = BX * BY
    owned_count = model_blocks.shape[0]
    pair_count = devices_all * cap_rows
    chooser = jnp.logical_and(
        lookup.reshape(-1)[:, None] == jnp.arange(owned_count, dtype=lookup.dtype)[None, :],
        filled.reshape(-1)[:, None],
    )
    table = jnp.concatenate(
        [
            model_blocks.reshape(owned_count, block_rows * BZ),
            jnp.broadcast_to(block_scales[:, None], (owned_count, BZ)),
        ],
        axis=1,
    )
    payload = jnp.dot(chooser.astype(table.dtype), table, preferred_element_type=jnp.float32)
    payload = payload.astype(model_blocks.dtype).reshape(devices_all, cap_rows, block_rows + 1, BZ)
    arrived = lax.all_to_all(payload, ("shot", "blk"), split_axis=0, concat_axis=0, tiled=True)

    my_owners = lax.dynamic_index_in_dim(owner_table, my_index, 0, keepdims=False)
    earlier = jnp.arange(slot_count)[None, :] < jnp.arange(slot_count)[:, None]
    my_ranks = jnp.sum(
        jnp.logical_and(my_owners[:, None] == my_owners[None, :], earlier).astype(jnp.int32), axis=1
    )
    flat_slot = my_owners * cap_rows + my_ranks
    slot_pick = flat_slot[:, None] == jnp.arange(pair_count, dtype=flat_slot.dtype)[None, :]
    rows = jnp.dot(
        slot_pick.astype(arrived.dtype), arrived.reshape(pair_count, (block_rows + 1) * BZ),
        preferred_element_type=jnp.float32,
    ).reshape(slot_count, block_rows + 1, BZ)
    values = rows[:, :block_rows].reshape((slot_count,) + block_shape)
    gain_rows = rows[:, block_rows, 0]
    scaled = values * gain_rows[:, None, None, None]
    courant = to_piece(scaled * scaled)
    (c_ext,) = extend_all([(courant, halo)])

    source_x = source_cell[0] // plane - blk_index * own
    source_rest = source_cell[0] % plane
    source_y = source_rest // size_z
    source_z = source_rest % size_z
    record = observed[0, 0]
    own_pick = one_hot_rows(listen // size_z, own * size_y)
    own_z = one_hot_rows(listen % size_z, size_z)

    snapshots = []
    misfit = []
    u_off, b_off = halo, halo - 4
    for step_index in range(STEPS):
        if step_index > 0 and step_index % GROUP == 0:
            u_ext, b_ext = extend_all([(crop(u_ext, u_off, 0, own), halo), (crop(b_ext, b_off, 0, own), halo - 4)])
            u_off, b_off = halo, halo - 4
        new_off = u_off - 4
        curved = lap_valid(u_ext)
        snapshots.append(crop(curved, new_off, 0, own))
        advanced = (
            2.0 * crop(u_ext, u_off, new_off, own)
            - crop(b_ext, b_off, new_off, own)
            + crop(c_ext, halo, new_off, own) * curved
        )
        shape_now = advanced.shape
        at_source = (
            (lax.broadcasted_iota(jnp.int32, shape_now, 0) == source_x + new_off)
            & (lax.broadcasted_iota(jnp.int32, shape_now, 1) == source_y)
            & (lax.broadcasted_iota(jnp.int32, shape_now, 2) == source_z)
        )
        advanced = advanced + jnp.where(at_source, wavelet[0, step_index], jnp.zeros((), jnp.float32))
        sampled = pick_dot(own_pick, crop(advanced, new_off, 0, own).reshape(own * size_y, size_z))
        misfit.append(jnp.sum(sampled * own_z, axis=1) - record[step_index])
        b_ext, b_off = u_ext, u_off
        u_ext, u_off = advanced, new_off
    field_end = crop(u_ext, u_off, 0, own)

    misfit_all = jnp.stack(misfit)
    misfit_all, adjoint_from_left, adjoint_from_right = lax.optimization_barrier(
        (misfit_all, adjoint_from_left, adjoint_from_right)
    )
    m_ext, l_ext = [
        jnp.concatenate([left, cells, right], axis=0)
        for (cells, _), left, right in zip(
            adjoint_fields,
            unpack(adjoint_from_left, adjoint_tails),
            unpack(adjoint_from_right, adjoint_heads),
        )
    ]
    (misfit_left,), (misfit_right,) = swap([misfit_all], [misfit_all])
    misfit_ext = jnp.concatenate([misfit_left, misfit_all, misfit_right], axis=1)
    cells_all = jnp.concatenate([listen_left, listen, listen_right])
    shift_all = jnp.concatenate(
        [
            jnp.full(listen.shape, -own, jnp.int32),
            jnp.zeros(listen.shape, jnp.int32),
            jnp.full(listen.shape, own, jnp.int32),
        ]
    )
    rec_x = cells_all // plane + shift_all + halo
    rec_plane = jnp.where(
        jnp.logical_and(rec_x >= 0, rec_x < own + 2 * halo), rec_x * size_y + (cells_all % plane) // size_z, -1
    )
    rec_pick = (
        jnp.arange((own + 2 * halo) * size_y, dtype=jnp.int32)[:, None] == rec_plane[None, :]
    ).astype(jnp.float32)
    rec_z = one_hot_rows(cells_all % size_z, size_z)

    m_off, l_off = halo, halo - 4
    gradient_field = jnp.zeros_like(adjoint_next)
    for count_index, step_index in enumerate(range(STEPS - 1, -1, -1)):
        if count_index > 0 and count_index % GROUP == 0:
            m_ext, l_ext = extend_all([(crop(m_ext, m_off, 0, own), halo), (crop(l_ext, l_off, 0, own), halo - 4)])
            m_off, l_off = halo, halo - 4
        new_off = m_off - 4
        adjoint = (
            2.0 * crop(m_ext, m_off, new_off, own)
            - crop(l_ext, l_off, new_off, own)
            + lap_valid(crop(c_ext, halo, m_off, own) * m_ext)
        )
        shape_now = adjoint.shape
        first_row = (halo - new_off) * size_y
        pick_now = rec_pick[first_row : first_row + shape_now[0] * size_y]
        injected = pick_dot(pick_now, rec_z * misfit_ext[step_index][:, None])
        adjoint = adjoint + injected.reshape(shape_now)
        gradient_field = gradient_field + crop(adjoint, new_off, 0, own) * snapshots[step_index]
        l_ext, l_off = m_ext, m_off
        m_ext, m_off = adjoint, new_off
    adjoint_first = crop(m_ext, m_off, 0, own)

    partial_blocks = to_blocks(GRADIENT_GAIN * gradient_field).reshape(slot_count, block_rows, BZ)
    parcel = exact_dot(slot_pick.T.astype(jnp.float32), partial_blocks.reshape(slot_count, block_rows * BZ))
    parcel = parcel.reshape(devices_all, cap_rows, block_rows, BZ)
    returned = lax.all_to_all(parcel, ("shot", "blk"), split_axis=0, concat_axis=0, tiled=True)
    gradient = exact_dot(chooser.T.astype(jnp.float32), returned.reshape(pair_count, -1)).reshape(model_blocks.shape)
    return (gradient, field_end[None], adjoint_first[None])


def solution(mesh):
    in_specs = (
        P(("shot", "blk"), None, None, None),
        P(("shot", "blk")),
        P(),
        P(),
        P("shot"),
        P("shot", None),
        P("shot", "blk", None),
        P("shot", "blk", None, None),
        P("shot", "blk", None, None),
        P("shot", "blk", None, None),
        P("shot", "blk", None, None),
        P("shot", "blk", None, None),
    )
    out_specs = (
        P(("shot", "blk"), None, None, None),
        P("shot", "blk", None, None),
        P("shot", "blk", None, None),
    )

    return jax.shard_map(local, mesh=mesh, in_specs=in_specs, out_specs=out_specs, check_vma=False)
```

```python
import jax
import jax.numpy as jnp
from jax import lax
from jax.sharding import PartitionSpec as P


BX = 2
BY = 4
BZ = 128
KX = 16
KY = 8
STEPS = 8
GROUP = 4


COEFFS = (-205.0 / 72.0, 8.0 / 5.0, -1.0 / 5.0, 8.0 / 315.0, -1.0 / 560.0)
GRADIENT_GAIN = 0.0625


def from_left(x):
    count = lax.axis_size("blk")
    return lax.ppermute(x, "blk", [(i, i + 1) for i in range(count - 1)])


def from_right(x):
    count = lax.axis_size("blk")
    return lax.ppermute(x, "blk", [(i + 1, i) for i in range(count - 1)])


def pack(parts):
    return jnp.concatenate([part.reshape(-1, part.shape[-1]) for part in parts], axis=0)


def unpack(buffer, likes):
    pieces, start = [], 0
    for like in likes:
        rows = like.size // like.shape[-1]
        pieces.append(buffer[start : start + rows].reshape(like.shape))
        start += rows
    return pieces


def swap(to_right, to_left):
    got_left = unpack(from_left(pack(to_right)), to_right)
    got_right = unpack(from_right(pack(to_left)), to_left)
    return got_left, got_right


def extend_all(fields):
    tails = [cells[cells.shape[0] - width :] for cells, width in fields]
    heads = [cells[:width] for cells, width in fields]
    got_left, got_right = swap(tails, heads)
    return [
        jnp.concatenate([left, cells, right], axis=0)
        for (cells, _), left, right in zip(fields, got_left, got_right)
    ]


def crop(cells, offset, want, own):
    start = offset - want
    return cells[start : start + own + 2 * want]


def lap_valid(cells):
    extent = (cells.shape[0] - 8, cells.shape[1], cells.shape[2])
    padded = jnp.pad(cells, ((0, 0), (4, 4), (4, 4)))
    centre = padded[4 : 4 + extent[0], 4 : 4 + extent[1], 4 : 4 + extent[2]]
    summed = 3.0 * COEFFS[0] * centre
    for offset in range(1, 5):
        beside_all = (
            padded[4 + offset : 4 + offset + extent[0], 4 : 4 + extent[1], 4 : 4 + extent[2]]
            + padded[4 - offset : 4 - offset + extent[0], 4 : 4 + extent[1], 4 : 4 + extent[2]]
            + padded[4 : 4 + extent[0], 4 + offset : 4 + offset + extent[1], 4 : 4 + extent[2]]
            + padded[4 : 4 + extent[0], 4 - offset : 4 - offset + extent[1], 4 : 4 + extent[2]]
            + padded[4 : 4 + extent[0], 4 : 4 + extent[1], 4 + offset : 4 + offset + extent[2]]
            + padded[4 : 4 + extent[0], 4 : 4 + extent[1], 4 - offset : 4 - offset + extent[2]]
        )
        summed = summed + COEFFS[offset] * beside_all
    return summed


def to_piece(blocks):
    return blocks.reshape(KX, KY, BX, BY, BZ).transpose(0, 2, 1, 3, 4).reshape(KX * BX, KY * BY, BZ)


def to_blocks(field_piece):
    return (
        field_piece.reshape(KX, BX, KY, BY, BZ)
        .transpose(0, 2, 1, 3, 4)
        .reshape(KX * KY, BX, BY, BZ)
    )


def one_hot_rows(index, count):
    return (index[:, None] == jnp.arange(count, dtype=index.dtype)[None, :]).astype(jnp.float32)


def exact_dot(left, right):
    return jnp.dot(left, right, precision=lax.Precision.HIGHEST, preferred_element_type=jnp.float32)


def pick_dot(one_hot, values):
    return jnp.dot(one_hot, values, precision=lax.Precision.HIGH, preferred_element_type=jnp.float32)


def local(
    model_blocks,
    block_scales,
    aperture_owner,
    aperture_local,
    source_cell,
    wavelet,
    receiver_cell,
    observed,
    field_now,
    field_change,
    adjoint_last,
    adjoint_change,
):
    devices_all = lax.axis_size(("shot", "blk"))
    my_index = lax.axis_index(("shot", "blk"))
    blk_index = lax.axis_index("blk")
    slot_count = aperture_local.shape[0] // devices_all
    cap_rows = 2
    halo = 4 * GROUP

    own, size_y, size_z = field_now.shape[1:]
    plane = size_y * size_z
    listen = receiver_cell[0, 0]
    current = field_now[0]
    before = current - field_change[0]
    first_fields = [(current, halo), (before, halo - 4)]
    tails = [cells[own - width :] for cells, width in first_fields]
    heads = [cells[:width] for cells, width in first_fields]
    to_right, to_left = pack(tails), pack(heads)
    got_left = unpack(from_left(to_right), tails)
    got_right = unpack(from_right(to_left), heads)
    u_ext, b_ext = [
        jnp.concatenate([left, cells, right], axis=0)
        for (cells, _), left, right in zip(first_fields, got_left, got_right)
    ]
    adjoint_next = adjoint_last[0]
    latest = adjoint_next - adjoint_change[0]

    owner_table = aperture_owner[:, 0].reshape(devices_all, slot_count)
    local_table = aperture_local.reshape(devices_all, slot_count)
    picked = owner_table == my_index
    count = jnp.sum(picked.astype(jnp.int32), axis=1)
    first = jnp.argmax(picked, axis=1)
    last = slot_count - 1 - jnp.argmax(picked[:, ::-1], axis=1)
    slot_iota = jnp.arange(slot_count, dtype=first.dtype)[None, :]
    lookup = jnp.stack(
        [
            jnp.sum(jnp.where(slot_iota == first[:, None], local_table, 0), axis=1),
            jnp.sum(jnp.where(slot_iota == last[:, None], local_table, 0), axis=1),
        ],
        axis=1,
    )
    filled = jnp.stack([count >= 1, count >= 2], axis=1)
    block_shape = model_blocks.shape[1:]
    block_rows = BX * BY
    owned_count = model_blocks.shape[0]
    pair_count = devices_all * cap_rows
    chooser = jnp.logical_and(
        lookup.reshape(-1)[:, None] == jnp.arange(owned_count, dtype=lookup.dtype)[None, :],
        filled.reshape(-1)[:, None],
    )
    table = jnp.concatenate(
        [
            model_blocks.reshape(owned_count, block_rows * BZ),
            jnp.broadcast_to(block_scales[:, None], (owned_count, BZ)),
        ],
        axis=1,
    )
    payload = jnp.dot(chooser.astype(table.dtype), table, preferred_element_type=jnp.float32)
    payload = payload.astype(model_blocks.dtype).reshape(devices_all, cap_rows, block_rows + 1, BZ)
    arrived = lax.all_to_all(payload, ("shot", "blk"), split_axis=0, concat_axis=0, tiled=True)

    my_owners = lax.dynamic_index_in_dim(owner_table, my_index, 0, keepdims=False)
    earlier = jnp.arange(slot_count)[None, :] < jnp.arange(slot_count)[:, None]
    my_ranks = jnp.sum(
        jnp.logical_and(my_owners[:, None] == my_owners[None, :], earlier).astype(jnp.int32), axis=1
    )
    flat_slot = my_owners * cap_rows + my_ranks
    slot_pick = flat_slot[:, None] == jnp.arange(pair_count, dtype=flat_slot.dtype)[None, :]
    rows = jnp.dot(
        slot_pick.astype(arrived.dtype), arrived.reshape(pair_count, (block_rows + 1) * BZ),
        preferred_element_type=jnp.float32,
    ).reshape(slot_count, block_rows + 1, BZ)
    values = rows[:, :block_rows].reshape((slot_count,) + block_shape)
    gain_rows = rows[:, block_rows, 0]
    scaled = values * gain_rows[:, None, None, None]
    courant = to_piece(scaled * scaled)
    (c_ext,) = extend_all([(courant, halo)])

    source_x = source_cell[0] // plane - blk_index * own
    source_rest = source_cell[0] % plane
    source_y = source_rest // size_z
    source_z = source_rest % size_z
    record = observed[0, 0]
    own_pick = one_hot_rows(listen // size_z, own * size_y)
    own_z = one_hot_rows(listen % size_z, size_z)

    snapshots = []
    misfit = []
    u_off, b_off = halo, halo - 4
    for step_index in range(STEPS):
        if step_index > 0 and step_index % GROUP == 0:
            u_ext, b_ext = extend_all([(crop(u_ext, u_off, 0, own), halo), (crop(b_ext, b_off, 0, own), halo - 4)])
            u_off, b_off = halo, halo - 4
        new_off = u_off - 4
        curved = lap_valid(u_ext)
        snapshots.append(crop(curved, new_off, 0, own))
        advanced = (
            2.0 * crop(u_ext, u_off, new_off, own)
            - crop(b_ext, b_off, new_off, own)
            + crop(c_ext, halo, new_off, own) * curved
        )
        shape_now = advanced.shape
        at_source = (
            (lax.broadcasted_iota(jnp.int32, shape_now, 0) == source_x + new_off)
            & (lax.broadcasted_iota(jnp.int32, shape_now, 1) == source_y)
            & (lax.broadcasted_iota(jnp.int32, shape_now, 2) == source_z)
        )
        advanced = advanced + jnp.where(at_source, wavelet[0, step_index], jnp.zeros((), jnp.float32))
        sampled = pick_dot(own_pick, crop(advanced, new_off, 0, own).reshape(own * size_y, size_z))
        misfit.append(jnp.sum(sampled * own_z, axis=1) - record[step_index])
        b_ext, b_off = u_ext, u_off
        u_ext, u_off = advanced, new_off
    field_end = crop(u_ext, u_off, 0, own)

    misfit_all = jnp.stack(misfit)
    listen_row = listen.astype(jnp.float32)[None, :]
    adjoint_fields = [(adjoint_next, halo), (latest, halo - 4)]
    adjoint_tails = [cells[own - width :] for cells, width in adjoint_fields] + [misfit_all, listen_row]
    adjoint_heads = [cells[:width] for cells, width in adjoint_fields] + [misfit_all, listen_row]
    got_left, got_right = swap(adjoint_tails, adjoint_heads)
    m_ext, l_ext = [
        jnp.concatenate([left, cells, right], axis=0)
        for (cells, _), left, right in zip(adjoint_fields, got_left, got_right)
    ]
    misfit_ext = jnp.concatenate([got_left[2], misfit_all, got_right[2]], axis=1)
    listen_left = got_left[3][0].astype(jnp.int32)
    listen_right = got_right[3][0].astype(jnp.int32)
    cells_all = jnp.concatenate([listen_left, listen, listen_right])
    shift_all = jnp.concatenate(
        [
            jnp.full(listen.shape, -own, jnp.int32),
            jnp.zeros(listen.shape, jnp.int32),
            jnp.full(listen.shape, own, jnp.int32),
        ]
    )
    rec_x = cells_all // plane + shift_all + halo
    rec_plane = jnp.where(
        jnp.logical_and(rec_x >= 0, rec_x < own + 2 * halo), rec_x * size_y + (cells_all % plane) // size_z, -1
    )
    rec_pick = (
        jnp.arange((own + 2 * halo) * size_y, dtype=jnp.int32)[:, None] == rec_plane[None, :]
    ).astype(jnp.float32)
    rec_z = one_hot_rows(cells_all % size_z, size_z)

    m_off, l_off = halo, halo - 4
    gradient_field = jnp.zeros_like(adjoint_next)
    for count_index, step_index in enumerate(range(STEPS - 1, -1, -1)):
        if count_index > 0 and count_index % GROUP == 0:
            m_ext, l_ext = extend_all([(crop(m_ext, m_off, 0, own), halo), (crop(l_ext, l_off, 0, own), halo - 4)])
            m_off, l_off = halo, halo - 4
        new_off = m_off - 4
        adjoint = (
            2.0 * crop(m_ext, m_off, new_off, own)
            - crop(l_ext, l_off, new_off, own)
            + lap_valid(crop(c_ext, halo, m_off, own) * m_ext)
        )
        shape_now = adjoint.shape
        first_row = (halo - new_off) * size_y
        pick_now = rec_pick[first_row : first_row + shape_now[0] * size_y]
        injected = pick_dot(pick_now, rec_z * misfit_ext[step_index][:, None])
        adjoint = adjoint + injected.reshape(shape_now)
        gradient_field = gradient_field + crop(adjoint, new_off, 0, own) * snapshots[step_index]
        l_ext, l_off = m_ext, m_off
        m_ext, m_off = adjoint, new_off
    adjoint_first = crop(m_ext, m_off, 0, own)

    partial_blocks = to_blocks(GRADIENT_GAIN * gradient_field).reshape(slot_count, block_rows, BZ)
    parcel = exact_dot(slot_pick.T.astype(jnp.float32), partial_blocks.reshape(slot_count, block_rows * BZ))
    parcel = parcel.reshape(devices_all, cap_rows, block_rows, BZ)
    returned = lax.all_to_all(parcel, ("shot", "blk"), split_axis=0, concat_axis=0, tiled=True)
    gradient = exact_dot(chooser.T.astype(jnp.float32), returned.reshape(pair_count, -1)).reshape(model_blocks.shape)
    return (gradient, field_end[None], adjoint_first[None])


def solution(mesh):
    in_specs = (
        P(("shot", "blk"), None, None, None),
        P(("shot", "blk")),
        P(),
        P(),
        P("shot"),
        P("shot", None),
        P("shot", "blk", None),
        P("shot", "blk", None, None),
        P("shot", "blk", None, None),
        P("shot", "blk", None, None),
        P("shot", "blk", None, None),
        P("shot", "blk", None, None),
    )
    out_specs = (
        P(("shot", "blk"), None, None, None),
        P("shot", "blk", None, None),
        P("shot", "blk", None, None),
    )

    return jax.shard_map(local, mesh=mesh, in_specs=in_specs, out_specs=out_specs, check_vma=False)
```

```python
import jax
import jax.numpy as jnp
from jax import lax
from jax.sharding import PartitionSpec as P


BX = 2
BY = 4
BZ = 128
KX = 16
KY = 8
STEPS = 8
GROUP = 4


COEFFS = (-205.0 / 72.0, 8.0 / 5.0, -1.0 / 5.0, 8.0 / 315.0, -1.0 / 560.0)
GRADIENT_GAIN = 0.0625


def from_left(x):
    count = lax.axis_size("blk")
    return lax.ppermute(x, "blk", [(i, i + 1) for i in range(count - 1)])


def from_right(x):
    count = lax.axis_size("blk")
    return lax.ppermute(x, "blk", [(i + 1, i) for i in range(count - 1)])


def pack(parts):
    return jnp.concatenate([part.reshape(-1, part.shape[-1]) for part in parts], axis=0)


def unpack(buffer, likes):
    pieces, start = [], 0
    for like in likes:
        rows = like.size // like.shape[-1]
        pieces.append(buffer[start : start + rows].reshape(like.shape))
        start += rows
    return pieces


def swap(to_right, to_left):
    got_left = unpack(from_left(pack(to_right)), to_right)
    got_right = unpack(from_right(pack(to_left)), to_left)
    return got_left, got_right


def extend_all(fields):
    tails = [cells[cells.shape[0] - width :] for cells, width in fields]
    heads = [cells[:width] for cells, width in fields]
    got_left, got_right = swap(tails, heads)
    return [
        jnp.concatenate([left, cells, right], axis=0)
        for (cells, _), left, right in zip(fields, got_left, got_right)
    ]


def crop(cells, offset, want, own):
    start = offset - want
    return cells[start : start + own + 2 * want]


def lap_valid(cells):
    extent = (cells.shape[0] - 8, cells.shape[1], cells.shape[2])
    padded = jnp.pad(cells, ((0, 0), (4, 4), (4, 4)))
    centre = padded[4 : 4 + extent[0], 4 : 4 + extent[1], 4 : 4 + extent[2]]
    summed = 3.0 * COEFFS[0] * centre
    for offset in range(1, 5):
        beside_all = (
            padded[4 + offset : 4 + offset + extent[0], 4 : 4 + extent[1], 4 : 4 + extent[2]]
            + padded[4 - offset : 4 - offset + extent[0], 4 : 4 + extent[1], 4 : 4 + extent[2]]
            + padded[4 : 4 + extent[0], 4 + offset : 4 + offset + extent[1], 4 : 4 + extent[2]]
            + padded[4 : 4 + extent[0], 4 - offset : 4 - offset + extent[1], 4 : 4 + extent[2]]
            + padded[4 : 4 + extent[0], 4 : 4 + extent[1], 4 + offset : 4 + offset + extent[2]]
            + padded[4 : 4 + extent[0], 4 : 4 + extent[1], 4 - offset : 4 - offset + extent[2]]
        )
        summed = summed + COEFFS[offset] * beside_all
    return summed


def to_piece(blocks):
    return blocks.reshape(KX, KY, BX, BY, BZ).transpose(0, 2, 1, 3, 4).reshape(KX * BX, KY * BY, BZ)


def to_blocks(field_piece):
    return (
        field_piece.reshape(KX, BX, KY, BY, BZ)
        .transpose(0, 2, 1, 3, 4)
        .reshape(KX * KY, BX, BY, BZ)
    )


def one_hot_rows(index, count):
    return (index[:, None] == jnp.arange(count, dtype=index.dtype)[None, :]).astype(jnp.float32)


def exact_dot(left, right):
    return jnp.dot(left, right, precision=lax.Precision.HIGHEST, preferred_element_type=jnp.float32)


def pick_dot(one_hot, values):
    return jnp.dot(one_hot, values, precision=lax.Precision.HIGH, preferred_element_type=jnp.float32)


def local(
    model_blocks,
    block_scales,
    aperture_owner,
    aperture_local,
    source_cell,
    wavelet,
    receiver_cell,
    observed,
    field_now,
    field_change,
    adjoint_last,
    adjoint_change,
):
    devices_all = lax.axis_size(("shot", "blk"))
    my_index = lax.axis_index(("shot", "blk"))
    blk_index = lax.axis_index("blk")
    slot_count = aperture_local.shape[0] // devices_all
    cap_rows = 2
    halo = 4 * GROUP

    own, size_y, size_z = field_now.shape[1:]
    plane = size_y * size_z
    listen = receiver_cell[0, 0]
    current = field_now[0]
    before = current - field_change[0]
    listen_row = listen.astype(jnp.float32)[None, :]
    first_fields = [(current, halo), (before, halo - 4)]
    tails = [cells[own - width :] for cells, width in first_fields] + [listen_row]
    heads = [cells[:width] for cells, width in first_fields] + [listen_row]
    to_right, to_left = pack(tails), pack(heads)
    got_left = unpack(from_left(to_right), tails)
    got_right = unpack(from_right(to_left), heads)
    u_ext, b_ext = [
        jnp.concatenate([left, cells, right], axis=0)
        for (cells, _), left, right in zip(first_fields, got_left, got_right)
    ]
    adjoint_next = adjoint_last[0]
    latest = adjoint_next - adjoint_change[0]
    adjoint_fields = [(adjoint_next, halo), (latest, halo - 4)]
    adjoint_tails = [cells[own - width :] for cells, width in adjoint_fields]
    adjoint_heads = [cells[:width] for cells, width in adjoint_fields]
    adjoint_from_left = from_left(pack(adjoint_tails))
    adjoint_from_right = from_right(pack(adjoint_heads))
    listen_left = got_left[-1][0].astype(jnp.int32)
    listen_right = got_right[-1][0].astype(jnp.int32)

    owner_table = aperture_owner[:, 0].reshape(devices_all, slot_count)
    local_table = aperture_local.reshape(devices_all, slot_count)
    picked = owner_table == my_index
    count = jnp.sum(picked.astype(jnp.int32), axis=1)
    first = jnp.argmax(picked, axis=1)
    last = slot_count - 1 - jnp.argmax(picked[:, ::-1], axis=1)
    slot_iota = jnp.arange(slot_count, dtype=first.dtype)[None, :]
    lookup = jnp.stack(
        [
            jnp.sum(jnp.where(slot_iota == first[:, None], local_table, 0), axis=1),
            jnp.sum(jnp.where(slot_iota == last[:, None], local_table, 0), axis=1),
        ],
        axis=1,
    )
    filled = jnp.stack([count >= 1, count >= 2], axis=1)
    block_shape = model_blocks.shape[1:]
    block_rows = BX * BY
    owned_count = model_blocks.shape[0]
    pair_count = devices_all * cap_rows
    chooser = jnp.logical_and(
        lookup.reshape(-1)[:, None] == jnp.arange(owned_count, dtype=lookup.dtype)[None, :],
        filled.reshape(-1)[:, None],
    )
    table = jnp.concatenate(
        [
            model_blocks.reshape(owned_count, block_rows * BZ),
            jnp.broadcast_to(block_scales[:, None], (owned_count, BZ)),
        ],
        axis=1,
    )
    payload = jnp.dot(chooser.astype(table.dtype), table, preferred_element_type=jnp.float32)
    payload = payload.astype(model_blocks.dtype).reshape(devices_all, cap_rows, block_rows + 1, BZ)
    arrived = lax.all_to_all(payload, ("shot", "blk"), split_axis=0, concat_axis=0, tiled=True)

    my_owners = lax.dynamic_index_in_dim(owner_table, my_index, 0, keepdims=False)
    earlier = jnp.arange(slot_count)[None, :] < jnp.arange(slot_count)[:, None]
    my_ranks = jnp.sum(
        jnp.logical_and(my_owners[:, None] == my_owners[None, :], earlier).astype(jnp.int32), axis=1
    )
    flat_slot = my_owners * cap_rows + my_ranks
    slot_pick = flat_slot[:, None] == jnp.arange(pair_count, dtype=flat_slot.dtype)[None, :]
    rows = jnp.dot(
        slot_pick.astype(arrived.dtype), arrived.reshape(pair_count, (block_rows + 1) * BZ),
        preferred_element_type=jnp.float32,
    ).reshape(slot_count, block_rows + 1, BZ)
    values = rows[:, :block_rows].reshape((slot_count,) + block_shape)
    gain_rows = rows[:, block_rows, 0]
    scaled = values * gain_rows[:, None, None, None]
    courant = to_piece(scaled * scaled)
    (c_ext,) = extend_all([(courant, halo)])

    source_x = source_cell[0] // plane - blk_index * own
    source_rest = source_cell[0] % plane
    source_y = source_rest // size_z
    source_z = source_rest % size_z
    record = observed[0, 0]
    own_pick = one_hot_rows(listen // size_z, own * size_y)
    own_z = one_hot_rows(listen % size_z, size_z)

    snapshots = []
    misfit = []
    u_off, b_off = halo, halo - 4
    for step_index in range(STEPS):
        if step_index > 0 and step_index % GROUP == 0:
            u_ext, b_ext = extend_all([(crop(u_ext, u_off, 0, own), halo), (crop(b_ext, b_off, 0, own), halo - 4)])
            u_off, b_off = halo, halo - 4
        new_off = u_off - 4
        curved = lap_valid(u_ext)
        snapshots.append(crop(curved, new_off, 0, own))
        advanced = (
            2.0 * crop(u_ext, u_off, new_off, own)
            - crop(b_ext, b_off, new_off, own)
            + crop(c_ext, halo, new_off, own) * curved
        )
        shape_now = advanced.shape
        at_source = (
            (lax.broadcasted_iota(jnp.int32, shape_now, 0) == source_x + new_off)
            & (lax.broadcasted_iota(jnp.int32, shape_now, 1) == source_y)
            & (lax.broadcasted_iota(jnp.int32, shape_now, 2) == source_z)
        )
        advanced = advanced + jnp.where(at_source, wavelet[0, step_index], jnp.zeros((), jnp.float32))
        sampled = pick_dot(own_pick, crop(advanced, new_off, 0, own).reshape(own * size_y, size_z))
        misfit.append(jnp.sum(sampled * own_z, axis=1) - record[step_index])
        b_ext, b_off = u_ext, u_off
        u_ext, u_off = advanced, new_off
    field_end = crop(u_ext, u_off, 0, own)

    misfit_all = jnp.stack(misfit)
    misfit_all, adjoint_from_left, adjoint_from_right = lax.optimization_barrier(
        (misfit_all, adjoint_from_left, adjoint_from_right)
    )
    m_ext, l_ext = [
        jnp.concatenate([left, cells, right], axis=0)
        for (cells, _), left, right in zip(
            adjoint_fields,
            unpack(adjoint_from_left, adjoint_tails),
            unpack(adjoint_from_right, adjoint_heads),
        )
    ]
    blk_count = lax.axis_size("blk")
    gathered = lax.all_gather(misfit_all, "blk")
    zero_misfit = jnp.zeros_like(misfit_all)
    misfit_left = jnp.where(
        blk_index > 0, lax.dynamic_index_in_dim(gathered, jnp.maximum(blk_index - 1, 0), 0, keepdims=False), zero_misfit
    )
    misfit_right = jnp.where(
        blk_index < blk_count - 1,
        lax.dynamic_index_in_dim(gathered, jnp.minimum(blk_index + 1, blk_count - 1), 0, keepdims=False),
        zero_misfit,
    )
    misfit_ext = jnp.concatenate([misfit_left, misfit_all, misfit_right], axis=1)
    cells_all = jnp.concatenate([listen_left, listen, listen_right])
    shift_all = jnp.concatenate(
        [
            jnp.full(listen.shape, -own, jnp.int32),
            jnp.zeros(listen.shape, jnp.int32),
            jnp.full(listen.shape, own, jnp.int32),
        ]
    )
    rec_x = cells_all // plane + shift_all + halo
    rec_plane = jnp.where(
        jnp.logical_and(rec_x >= 0, rec_x < own + 2 * halo), rec_x * size_y + (cells_all % plane) // size_z, -1
    )
    rec_pick = (
        jnp.arange((own + 2 * halo) * size_y, dtype=jnp.int32)[:, None] == rec_plane[None, :]
    ).astype(jnp.float32)
    rec_z = one_hot_rows(cells_all % size_z, size_z)

    m_off, l_off = halo, halo - 4
    gradient_field = jnp.zeros_like(adjoint_next)
    for count_index, step_index in enumerate(range(STEPS - 1, -1, -1)):
        if count_index > 0 and count_index % GROUP == 0:
            m_ext, l_ext = extend_all([(crop(m_ext, m_off, 0, own), halo), (crop(l_ext, l_off, 0, own), halo - 4)])
            m_off, l_off = halo, halo - 4
        new_off = m_off - 4
        adjoint = (
            2.0 * crop(m_ext, m_off, new_off, own)
            - crop(l_ext, l_off, new_off, own)
            + lap_valid(crop(c_ext, halo, m_off, own) * m_ext)
        )
        shape_now = adjoint.shape
        first_row = (halo - new_off) * size_y
        pick_now = rec_pick[first_row : first_row + shape_now[0] * size_y]
        injected = pick_dot(pick_now, rec_z * misfit_ext[step_index][:, None])
        adjoint = adjoint + injected.reshape(shape_now)
        gradient_field = gradient_field + crop(adjoint, new_off, 0, own) * snapshots[step_index]
        l_ext, l_off = m_ext, m_off
        m_ext, m_off = adjoint, new_off
    adjoint_first = crop(m_ext, m_off, 0, own)

    partial_blocks = to_blocks(GRADIENT_GAIN * gradient_field).reshape(slot_count, block_rows, BZ)
    parcel = exact_dot(slot_pick.T.astype(jnp.float32), partial_blocks.reshape(slot_count, block_rows * BZ))
    parcel = parcel.reshape(devices_all, cap_rows, block_rows, BZ)
    returned = lax.all_to_all(parcel, ("shot", "blk"), split_axis=0, concat_axis=0, tiled=True)
    gradient = exact_dot(chooser.T.astype(jnp.float32), returned.reshape(pair_count, -1)).reshape(model_blocks.shape)
    return (gradient, field_end[None], adjoint_first[None])


def solution(mesh):
    in_specs = (
        P(("shot", "blk"), None, None, None),
        P(("shot", "blk")),
        P(),
        P(),
        P("shot"),
        P("shot", None),
        P("shot", "blk", None),
        P("shot", "blk", None, None),
        P("shot", "blk", None, None),
        P("shot", "blk", None, None),
        P("shot", "blk", None, None),
        P("shot", "blk", None, None),
    )
    out_specs = (
        P(("shot", "blk"), None, None, None),
        P("shot", "blk", None, None),
        P("shot", "blk", None, None),
    )

    return jax.shard_map(local, mesh=mesh, in_specs=in_specs, out_specs=out_specs, check_vma=False)
```

```python
import jax
import jax.numpy as jnp
from jax import lax
from jax.sharding import PartitionSpec as P


BX = 2
BY = 4
BZ = 128
KX = 16
KY = 8
STEPS = 8
GROUP = 4


COEFFS = (-205.0 / 72.0, 8.0 / 5.0, -1.0 / 5.0, 8.0 / 315.0, -1.0 / 560.0)
GRADIENT_GAIN = 0.0625


def from_left(x):
    count = lax.axis_size("blk")
    return lax.ppermute(x, "blk", [(i, i + 1) for i in range(count - 1)])


def from_right(x):
    count = lax.axis_size("blk")
    return lax.ppermute(x, "blk", [(i + 1, i) for i in range(count - 1)])


def pack(parts):
    return jnp.concatenate([part.reshape(-1, part.shape[-1]) for part in parts], axis=0)


def unpack(buffer, likes):
    pieces, start = [], 0
    for like in likes:
        rows = like.size // like.shape[-1]
        pieces.append(buffer[start : start + rows].reshape(like.shape))
        start += rows
    return pieces


def swap(to_right, to_left):
    got_left = unpack(from_left(pack(to_right)), to_right)
    got_right = unpack(from_right(pack(to_left)), to_left)
    return got_left, got_right


def extend_all(fields):
    tails = [cells[cells.shape[0] - width :] for cells, width in fields]
    heads = [cells[:width] for cells, width in fields]
    got_left, got_right = swap(tails, heads)
    return [
        jnp.concatenate([left, cells, right], axis=0)
        for (cells, _), left, right in zip(fields, got_left, got_right)
    ]


def crop(cells, offset, want, own):
    start = offset - want
    return cells[start : start + own + 2 * want]


def lap_valid(cells):
    extent = (cells.shape[0] - 8, cells.shape[1], cells.shape[2])
    padded = jnp.pad(cells, ((0, 0), (4, 4), (4, 4)))
    centre = padded[4 : 4 + extent[0], 4 : 4 + extent[1], 4 : 4 + extent[2]]
    summed = 3.0 * COEFFS[0] * centre
    for offset in range(1, 5):
        beside_all = (
            padded[4 + offset : 4 + offset + extent[0], 4 : 4 + extent[1], 4 : 4 + extent[2]]
            + padded[4 - offset : 4 - offset + extent[0], 4 : 4 + extent[1], 4 : 4 + extent[2]]
            + padded[4 : 4 + extent[0], 4 + offset : 4 + offset + extent[1], 4 : 4 + extent[2]]
            + padded[4 : 4 + extent[0], 4 - offset : 4 - offset + extent[1], 4 : 4 + extent[2]]
            + padded[4 : 4 + extent[0], 4 : 4 + extent[1], 4 + offset : 4 + offset + extent[2]]
            + padded[4 : 4 + extent[0], 4 : 4 + extent[1], 4 - offset : 4 - offset + extent[2]]
        )
        summed = summed + COEFFS[offset] * beside_all
    return summed


def to_piece(blocks):
    return blocks.reshape(KX, KY, BX, BY, BZ).transpose(0, 2, 1, 3, 4).reshape(KX * BX, KY * BY, BZ)


def to_blocks(field_piece):
    return (
        field_piece.reshape(KX, BX, KY, BY, BZ)
        .transpose(0, 2, 1, 3, 4)
        .reshape(KX * KY, BX, BY, BZ)
    )


def one_hot_rows(index, count):
    return (index[:, None] == jnp.arange(count, dtype=index.dtype)[None, :]).astype(jnp.float32)


def exact_dot(left, right):
    return jnp.dot(left, right, precision=lax.Precision.HIGHEST, preferred_element_type=jnp.float32)


def pick_dot(one_hot, values):
    return jnp.dot(one_hot, values, precision=lax.Precision.HIGH, preferred_element_type=jnp.float32)


def local(
    model_blocks,
    block_scales,
    aperture_owner,
    aperture_local,
    source_cell,
    wavelet,
    receiver_cell,
    observed,
    field_now,
    field_change,
    adjoint_last,
    adjoint_change,
):
    devices_all = lax.axis_size(("shot", "blk"))
    my_index = lax.axis_index(("shot", "blk"))
    blk_index = lax.axis_index("blk")
    slot_count = aperture_local.shape[0] // devices_all
    cap_rows = 2
    halo = 4 * GROUP

    own, size_y, size_z = field_now.shape[1:]
    plane = size_y * size_z
    listen = receiver_cell[0, 0]
    current = field_now[0]
    before = current - field_change[0]
    listen_row = listen.astype(jnp.float32)[None, :]
    first_fields = [(current, halo), (before, halo - 4)]
    tails = [cells[own - width :] for cells, width in first_fields] + [listen_row]
    heads = [cells[:width] for cells, width in first_fields] + [listen_row]
    to_right, to_left = pack(tails), pack(heads)
    got_left = unpack(from_left(to_right), tails)
    got_right = unpack(from_right(to_left), heads)
    u_ext, b_ext = [
        jnp.concatenate([left, cells, right], axis=0)
        for (cells, _), left, right in zip(first_fields, got_left, got_right)
    ]
    adjoint_next = adjoint_last[0]
    latest = adjoint_next - adjoint_change[0]
    adjoint_fields = [(adjoint_next, halo), (latest, halo - 4)]
    adjoint_tails = [cells[own - width :] for cells, width in adjoint_fields]
    adjoint_heads = [cells[:width] for cells, width in adjoint_fields]
    adjoint_from_left = from_left(pack(adjoint_tails))
    adjoint_from_right = from_right(pack(adjoint_heads))
    listen_left = got_left[-1][0].astype(jnp.int32)
    listen_right = got_right[-1][0].astype(jnp.int32)

    owner_table = aperture_owner[:, 0].reshape(devices_all, slot_count)
    local_table = aperture_local.reshape(devices_all, slot_count)
    picked = owner_table == my_index
    count = jnp.sum(picked.astype(jnp.int32), axis=1)
    first = jnp.argmax(picked, axis=1)
    last = slot_count - 1 - jnp.argmax(picked[:, ::-1], axis=1)
    slot_iota = jnp.arange(slot_count, dtype=first.dtype)[None, :]
    lookup = jnp.stack(
        [
            jnp.sum(jnp.where(slot_iota == first[:, None], local_table, 0), axis=1),
            jnp.sum(jnp.where(slot_iota == last[:, None], local_table, 0), axis=1),
        ],
        axis=1,
    )
    filled = jnp.stack([count >= 1, count >= 2], axis=1)
    block_shape = model_blocks.shape[1:]
    block_rows = BX * BY
    owned_count = model_blocks.shape[0]
    pair_count = devices_all * cap_rows
    chooser = jnp.logical_and(
        lookup.reshape(-1)[:, None] == jnp.arange(owned_count, dtype=lookup.dtype)[None, :],
        filled.reshape(-1)[:, None],
    )
    table = jnp.concatenate(
        [
            model_blocks.reshape(owned_count, block_rows * BZ),
            jnp.broadcast_to(block_scales[:, None], (owned_count, BZ)),
        ],
        axis=1,
    )
    payload = jnp.dot(chooser.astype(table.dtype), table, preferred_element_type=jnp.float32)
    payload = payload.astype(model_blocks.dtype).reshape(devices_all, cap_rows, block_rows + 1, BZ)
    arrived = lax.all_to_all(payload, ("shot", "blk"), split_axis=0, concat_axis=0, tiled=True)

    my_owners = lax.dynamic_index_in_dim(owner_table, my_index, 0, keepdims=False)
    earlier = jnp.arange(slot_count)[None, :] < jnp.arange(slot_count)[:, None]
    my_ranks = jnp.sum(
        jnp.logical_and(my_owners[:, None] == my_owners[None, :], earlier).astype(jnp.int32), axis=1
    )
    flat_slot = my_owners * cap_rows + my_ranks
    slot_pick = flat_slot[:, None] == jnp.arange(pair_count, dtype=flat_slot.dtype)[None, :]
    rows = jnp.dot(
        slot_pick.astype(arrived.dtype), arrived.reshape(pair_count, (block_rows + 1) * BZ),
        preferred_element_type=jnp.float32,
    ).reshape(slot_count, block_rows + 1, BZ)
    values = rows[:, :block_rows].reshape((slot_count,) + block_shape)
    gain_rows = rows[:, block_rows, 0]
    scaled = values * gain_rows[:, None, None, None]
    courant = to_piece(scaled * scaled)
    (c_ext,) = extend_all([(courant, halo)])

    source_x = source_cell[0] // plane - blk_index * own
    source_rest = source_cell[0] % plane
    source_y = source_rest // size_z
    source_z = source_rest % size_z
    record = observed[0, 0]
    own_pick = one_hot_rows(listen // size_z, own * size_y)
    own_z = one_hot_rows(listen % size_z, size_z)

    snapshots = []
    misfit = []
    u_off, b_off = halo, halo - 4
    for step_index in range(STEPS):
        if step_index > 0 and step_index % GROUP == 0:
            u_ext, b_ext = extend_all([(crop(u_ext, u_off, 0, own), halo), (crop(b_ext, b_off, 0, own), halo - 4)])
            u_off, b_off = halo, halo - 4
        new_off = u_off - 4
        curved = lap_valid(u_ext)
        snapshots.append(crop(curved, new_off, 0, own))
        advanced = (
            2.0 * crop(u_ext, u_off, new_off, own)
            - crop(b_ext, b_off, new_off, own)
            + crop(c_ext, halo, new_off, own) * curved
        )
        shape_now = advanced.shape
        at_source = (
            (lax.broadcasted_iota(jnp.int32, shape_now, 0) == source_x + new_off)
            & (lax.broadcasted_iota(jnp.int32, shape_now, 1) == source_y)
            & (lax.broadcasted_iota(jnp.int32, shape_now, 2) == source_z)
        )
        advanced = advanced + jnp.where(at_source, wavelet[0, step_index], jnp.zeros((), jnp.float32))
        misfit.append(crop(advanced, new_off, 0, own).reshape(own * size_y, size_z))
        b_ext, b_off = u_ext, u_off
        u_ext, u_off = advanced, new_off
    field_end = crop(u_ext, u_off, 0, own)

    sampled = pick_dot(own_pick, jnp.concatenate(misfit, axis=1)).reshape(-1, STEPS, size_z)
    misfit_all = jnp.sum(sampled * own_z[:, None, :], axis=2).T - record
    misfit_all, adjoint_from_left, adjoint_from_right = lax.optimization_barrier(
        (misfit_all, adjoint_from_left, adjoint_from_right)
    )
    m_ext, l_ext = [
        jnp.concatenate([left, cells, right], axis=0)
        for (cells, _), left, right in zip(
            adjoint_fields,
            unpack(adjoint_from_left, adjoint_tails),
            unpack(adjoint_from_right, adjoint_heads),
        )
    ]
    (misfit_left,), (misfit_right,) = swap([misfit_all], [misfit_all])
    misfit_ext = jnp.concatenate([misfit_left, misfit_all, misfit_right], axis=1)
    cells_all = jnp.concatenate([listen_left, listen, listen_right])
    shift_all = jnp.concatenate(
        [
            jnp.full(listen.shape, -own, jnp.int32),
            jnp.zeros(listen.shape, jnp.int32),
            jnp.full(listen.shape, own, jnp.int32),
        ]
    )
    rec_x = cells_all // plane + shift_all + halo
    rec_plane = jnp.where(
        jnp.logical_and(rec_x >= 0, rec_x < own + 2 * halo), rec_x * size_y + (cells_all % plane) // size_z, -1
    )
    rec_pick = (
        jnp.arange((own + 2 * halo) * size_y, dtype=jnp.int32)[:, None] == rec_plane[None, :]
    ).astype(jnp.float32)
    rec_z = one_hot_rows(cells_all % size_z, size_z)

    injected_all = pick_dot(
        rec_pick, (rec_z[None, :, :] * misfit_ext[:, :, None]).transpose(1, 0, 2).reshape(rec_z.shape[0], -1)
    ).reshape(rec_pick.shape[0], STEPS, size_z)
    m_off, l_off = halo, halo - 4
    gradient_field = jnp.zeros_like(adjoint_next)
    for count_index, step_index in enumerate(range(STEPS - 1, -1, -1)):
        if count_index > 0 and count_index % GROUP == 0:
            m_ext, l_ext = extend_all([(crop(m_ext, m_off, 0, own), halo), (crop(l_ext, l_off, 0, own), halo - 4)])
            m_off, l_off = halo, halo - 4
        new_off = m_off - 4
        adjoint = (
            2.0 * crop(m_ext, m_off, new_off, own)
            - crop(l_ext, l_off, new_off, own)
            + lap_valid(crop(c_ext, halo, m_off, own) * m_ext)
        )
        shape_now = adjoint.shape
        first_row = (halo - new_off) * size_y
        injected = injected_all[first_row : first_row + shape_now[0] * size_y, step_index]
        adjoint = adjoint + injected.reshape(shape_now)
        gradient_field = gradient_field + crop(adjoint, new_off, 0, own) * snapshots[step_index]
        l_ext, l_off = m_ext, m_off
        m_ext, m_off = adjoint, new_off
    adjoint_first = crop(m_ext, m_off, 0, own)

    partial_blocks = to_blocks(GRADIENT_GAIN * gradient_field).reshape(slot_count, block_rows, BZ)
    parcel = exact_dot(slot_pick.T.astype(jnp.float32), partial_blocks.reshape(slot_count, block_rows * BZ))
    parcel = parcel.reshape(devices_all, cap_rows, block_rows, BZ)
    returned = lax.all_to_all(parcel, ("shot", "blk"), split_axis=0, concat_axis=0, tiled=True)
    gradient = exact_dot(chooser.T.astype(jnp.float32), returned.reshape(pair_count, -1)).reshape(model_blocks.shape)
    return (gradient, field_end[None], adjoint_first[None])


def solution(mesh):
    in_specs = (
        P(("shot", "blk"), None, None, None),
        P(("shot", "blk")),
        P(),
        P(),
        P("shot"),
        P("shot", None),
        P("shot", "blk", None),
        P("shot", "blk", None, None),
        P("shot", "blk", None, None),
        P("shot", "blk", None, None),
        P("shot", "blk", None, None),
        P("shot", "blk", None, None),
    )
    out_specs = (
        P(("shot", "blk"), None, None, None),
        P("shot", "blk", None, None),
        P("shot", "blk", None, None),
    )

    return jax.shard_map(local, mesh=mesh, in_specs=in_specs, out_specs=out_specs, check_vma=False)
```

```python
import jax
import jax.numpy as jnp
from jax import lax
from jax.sharding import PartitionSpec as P


BX = 2
BY = 4
BZ = 128
KX = 16
KY = 8
STEPS = 8
GROUP = 4


COEFFS = (-205.0 / 72.0, 8.0 / 5.0, -1.0 / 5.0, 8.0 / 315.0, -1.0 / 560.0)
GRADIENT_GAIN = 0.0625


def from_left(x):
    count = lax.axis_size("blk")
    return lax.ppermute(x, "blk", [(i, i + 1) for i in range(count - 1)])


def from_right(x):
    count = lax.axis_size("blk")
    return lax.ppermute(x, "blk", [(i + 1, i) for i in range(count - 1)])


def pack(parts):
    return jnp.concatenate([part.reshape(-1, part.shape[-1]) for part in parts], axis=0)


def unpack(buffer, likes):
    pieces, start = [], 0
    for like in likes:
        rows = like.size // like.shape[-1]
        pieces.append(buffer[start : start + rows].reshape(like.shape))
        start += rows
    return pieces


def swap(to_right, to_left):
    got_left = unpack(from_left(pack(to_right)), to_right)
    got_right = unpack(from_right(pack(to_left)), to_left)
    return got_left, got_right


def extend_all(fields):
    tails = [cells[cells.shape[0] - width :] for cells, width in fields]
    heads = [cells[:width] for cells, width in fields]
    got_left, got_right = swap(tails, heads)
    return [
        jnp.concatenate([left, cells, right], axis=0)
        for (cells, _), left, right in zip(fields, got_left, got_right)
    ]


def crop(cells, offset, want, own):
    start = offset - want
    return cells[start : start + own + 2 * want]


def lap_valid(cells):
    extent = (cells.shape[0] - 8, cells.shape[1], cells.shape[2])
    padded = jnp.pad(cells, ((0, 0), (4, 4), (4, 4)))
    centre = padded[4 : 4 + extent[0], 4 : 4 + extent[1], 4 : 4 + extent[2]]
    summed = 3.0 * COEFFS[0] * centre
    for offset in range(1, 5):
        beside_all = (
            padded[4 + offset : 4 + offset + extent[0], 4 : 4 + extent[1], 4 : 4 + extent[2]]
            + padded[4 - offset : 4 - offset + extent[0], 4 : 4 + extent[1], 4 : 4 + extent[2]]
            + padded[4 : 4 + extent[0], 4 + offset : 4 + offset + extent[1], 4 : 4 + extent[2]]
            + padded[4 : 4 + extent[0], 4 - offset : 4 - offset + extent[1], 4 : 4 + extent[2]]
            + padded[4 : 4 + extent[0], 4 : 4 + extent[1], 4 + offset : 4 + offset + extent[2]]
            + padded[4 : 4 + extent[0], 4 : 4 + extent[1], 4 - offset : 4 - offset + extent[2]]
        )
        summed = summed + COEFFS[offset] * beside_all
    return summed


def to_piece(blocks):
    return blocks.reshape(KX, KY, BX, BY, BZ).transpose(0, 2, 1, 3, 4).reshape(KX * BX, KY * BY, BZ)


def to_blocks(field_piece):
    return (
        field_piece.reshape(KX, BX, KY, BY, BZ)
        .transpose(0, 2, 1, 3, 4)
        .reshape(KX * KY, BX, BY, BZ)
    )


def one_hot_rows(index, count):
    return (index[:, None] == jnp.arange(count, dtype=index.dtype)[None, :]).astype(jnp.float32)


def exact_dot(left, right):
    return jnp.dot(left, right, precision=lax.Precision.HIGHEST, preferred_element_type=jnp.float32)


def pick_dot(one_hot, values):
    return jnp.dot(one_hot, values, precision=lax.Precision.HIGH, preferred_element_type=jnp.float32)


def local(
    model_blocks,
    block_scales,
    aperture_owner,
    aperture_local,
    source_cell,
    wavelet,
    receiver_cell,
    observed,
    field_now,
    field_change,
    adjoint_last,
    adjoint_change,
):
    devices_all = lax.axis_size(("shot", "blk"))
    my_index = lax.axis_index(("shot", "blk"))
    blk_index = lax.axis_index("blk")
    slot_count = aperture_local.shape[0] // devices_all
    cap_rows = 2
    halo = 4 * GROUP

    own, size_y, size_z = field_now.shape[1:]
    plane = size_y * size_z
    listen = receiver_cell[0, 0]
    current = field_now[0]
    before = current - field_change[0]
    listen_row = listen.astype(jnp.float32)[None, :]
    first_fields = [(current, halo), (before, halo - 4)]
    tails = [cells[own - width :] for cells, width in first_fields] + [listen_row]
    heads = [cells[:width] for cells, width in first_fields] + [listen_row]
    to_right, to_left = pack(tails), pack(heads)
    got_left = unpack(from_left(to_right), tails)
    got_right = unpack(from_right(to_left), heads)
    u_ext, b_ext = [
        jnp.concatenate([left, cells, right], axis=0)
        for (cells, _), left, right in zip(first_fields, got_left, got_right)
    ]
    adjoint_next = adjoint_last[0]
    latest = adjoint_next - adjoint_change[0]
    adjoint_fields = [(adjoint_next, halo), (latest, halo - 4)]
    adjoint_tails = [cells[own - width :] for cells, width in adjoint_fields]
    adjoint_heads = [cells[:width] for cells, width in adjoint_fields]
    adjoint_from_left = from_left(pack(adjoint_tails))
    adjoint_from_right = from_right(pack(adjoint_heads))
    listen_left = got_left[-1][0].astype(jnp.int32)
    listen_right = got_right[-1][0].astype(jnp.int32)

    owner_table = aperture_owner[:, 0].reshape(devices_all, slot_count)
    local_table = aperture_local.reshape(devices_all, slot_count)
    picked = owner_table == my_index
    count = jnp.sum(picked.astype(jnp.int32), axis=1)
    first = jnp.argmax(picked, axis=1)
    last = slot_count - 1 - jnp.argmax(picked[:, ::-1], axis=1)
    slot_iota = jnp.arange(slot_count, dtype=first.dtype)[None, :]
    lookup = jnp.stack(
        [
            jnp.sum(jnp.where(slot_iota == first[:, None], local_table, 0), axis=1),
            jnp.sum(jnp.where(slot_iota == last[:, None], local_table, 0), axis=1),
        ],
        axis=1,
    )
    filled = jnp.stack([count >= 1, count >= 2], axis=1)
    block_shape = model_blocks.shape[1:]
    block_rows = BX * BY
    owned_count = model_blocks.shape[0]
    pair_count = devices_all * cap_rows
    chooser = jnp.logical_and(
        lookup.reshape(-1)[:, None] == jnp.arange(owned_count, dtype=lookup.dtype)[None, :],
        filled.reshape(-1)[:, None],
    )
    table = jnp.concatenate(
        [
            model_blocks.reshape(owned_count, block_rows * BZ),
            jnp.broadcast_to(block_scales[:, None], (owned_count, BZ)),
        ],
        axis=1,
    )
    payload = jnp.dot(chooser.astype(table.dtype), table, preferred_element_type=jnp.float32)
    payload = payload.astype(model_blocks.dtype).reshape(devices_all, cap_rows, block_rows + 1, BZ)
    arrived = lax.all_to_all(payload, ("shot", "blk"), split_axis=0, concat_axis=0, tiled=True)

    my_owners = lax.dynamic_index_in_dim(owner_table, my_index, 0, keepdims=False)
    earlier = jnp.arange(slot_count)[None, :] < jnp.arange(slot_count)[:, None]
    my_ranks = jnp.sum(
        jnp.logical_and(my_owners[:, None] == my_owners[None, :], earlier).astype(jnp.int32), axis=1
    )
    flat_slot = my_owners * cap_rows + my_ranks
    slot_pick = flat_slot[:, None] == jnp.arange(pair_count, dtype=flat_slot.dtype)[None, :]
    rows = jnp.dot(
        slot_pick.astype(arrived.dtype), arrived.reshape(pair_count, (block_rows + 1) * BZ),
        preferred_element_type=jnp.float32,
    ).reshape(slot_count, block_rows + 1, BZ)
    values = rows[:, :block_rows].reshape((slot_count,) + block_shape)
    gain_rows = rows[:, block_rows, 0]
    scaled = values * gain_rows[:, None, None, None]
    courant = to_piece(scaled * scaled)
    (c_ext,) = extend_all([(courant, halo)])

    source_x = source_cell[0] // plane - blk_index * own
    source_rest = source_cell[0] % plane
    source_y = source_rest // size_z
    source_z = source_rest % size_z
    record = observed[0, 0]
    own_pick = one_hot_rows(listen // size_z, own * size_y)
    own_z = one_hot_rows(listen % size_z, size_z)

    snapshots = []
    misfit = []
    u_off, b_off = halo, halo - 4
    for step_index in range(STEPS):
        if step_index > 0 and step_index % GROUP == 0:
            u_ext, b_ext = extend_all([(crop(u_ext, u_off, 0, own), halo), (crop(b_ext, b_off, 0, own), halo - 4)])
            u_off, b_off = halo, halo - 4
        new_off = u_off - 4
        curved = lap_valid(u_ext)
        snapshots.append(crop(curved, new_off, 0, own))
        advanced = (
            2.0 * crop(u_ext, u_off, new_off, own)
            - crop(b_ext, b_off, new_off, own)
            + crop(c_ext, halo, new_off, own) * curved
        )
        shape_now = advanced.shape
        at_source = (
            (lax.broadcasted_iota(jnp.int32, shape_now, 0) == source_x + new_off)
            & (lax.broadcasted_iota(jnp.int32, shape_now, 1) == source_y)
            & (lax.broadcasted_iota(jnp.int32, shape_now, 2) == source_z)
        )
        advanced = advanced + jnp.where(at_source, wavelet[0, step_index], jnp.zeros((), jnp.float32))
        misfit.append(crop(advanced, new_off, 0, own).reshape(own * size_y, size_z))
        b_ext, b_off = u_ext, u_off
        u_ext, u_off = advanced, new_off
    field_end = crop(u_ext, u_off, 0, own)

    sampled = pick_dot(own_pick, jnp.concatenate(misfit, axis=1)).reshape(-1, STEPS, size_z)
    misfit_all = jnp.sum(sampled * own_z[:, None, :], axis=2).T - record
    misfit_all, adjoint_from_left, adjoint_from_right = lax.optimization_barrier(
        (misfit_all, adjoint_from_left, adjoint_from_right)
    )
    m_ext, l_ext = [
        jnp.concatenate([left, cells, right], axis=0)
        for (cells, _), left, right in zip(
            adjoint_fields,
            unpack(adjoint_from_left, adjoint_tails),
            unpack(adjoint_from_right, adjoint_heads),
        )
    ]
    (misfit_left,), (misfit_right,) = swap([misfit_all], [misfit_all])
    misfit_ext = jnp.concatenate([misfit_left, misfit_all, misfit_right], axis=1)
    cells_all = jnp.concatenate([listen_left, listen, listen_right])
    shift_all = jnp.concatenate(
        [
            jnp.full(listen.shape, -own, jnp.int32),
            jnp.zeros(listen.shape, jnp.int32),
            jnp.full(listen.shape, own, jnp.int32),
        ]
    )
    rec_x = cells_all // plane + shift_all + halo
    rec_plane = jnp.where(
        jnp.logical_and(rec_x >= 0, rec_x < own + 2 * halo), rec_x * size_y + (cells_all % plane) // size_z, -1
    )
    rec_pick = (
        jnp.arange((own + 2 * halo) * size_y, dtype=jnp.int32)[:, None] == rec_plane[None, :]
    ).astype(jnp.float32)
    rec_z = one_hot_rows(cells_all % size_z, size_z)

    def injections(steps):
        values = (rec_z[None, :, :] * misfit_ext[steps, :, None]).transpose(1, 0, 2).reshape(rec_z.shape[0], -1)
        return pick_dot(rec_pick, values).reshape(rec_pick.shape[0], len(steps), size_z)

    injected_groups = {}
    m_off, l_off = halo, halo - 4
    gradient_field = jnp.zeros_like(adjoint_next)
    for count_index, step_index in enumerate(range(STEPS - 1, -1, -1)):
        if count_index > 0 and count_index % GROUP == 0:
            m_ext, l_ext = extend_all([(crop(m_ext, m_off, 0, own), halo), (crop(l_ext, l_off, 0, own), halo - 4)])
            m_off, l_off = halo, halo - 4
        new_off = m_off - 4
        adjoint = (
            2.0 * crop(m_ext, m_off, new_off, own)
            - crop(l_ext, l_off, new_off, own)
            + lap_valid(crop(c_ext, halo, m_off, own) * m_ext)
        )
        shape_now = adjoint.shape
        first_row = (halo - new_off) * size_y
        group_index = count_index // GROUP
        if group_index not in injected_groups:
            group_steps = list(range(STEPS - 1 - group_index * GROUP, STEPS - 1 - (group_index + 1) * GROUP, -1))
            injected_groups[group_index] = injections(group_steps)
        injected = injected_groups[group_index][first_row : first_row + shape_now[0] * size_y, count_index % GROUP]
        adjoint = adjoint + injected.reshape(shape_now)
        gradient_field = gradient_field + crop(adjoint, new_off, 0, own) * snapshots[step_index]
        l_ext, l_off = m_ext, m_off
        m_ext, m_off = adjoint, new_off
    adjoint_first = crop(m_ext, m_off, 0, own)

    partial_blocks = to_blocks(GRADIENT_GAIN * gradient_field).reshape(slot_count, block_rows, BZ)
    parcel = exact_dot(slot_pick.T.astype(jnp.float32), partial_blocks.reshape(slot_count, block_rows * BZ))
    parcel = parcel.reshape(devices_all, cap_rows, block_rows, BZ)
    returned = lax.all_to_all(parcel, ("shot", "blk"), split_axis=0, concat_axis=0, tiled=True)
    gradient = exact_dot(chooser.T.astype(jnp.float32), returned.reshape(pair_count, -1)).reshape(model_blocks.shape)
    return (gradient, field_end[None], adjoint_first[None])


def solution(mesh):
    in_specs = (
        P(("shot", "blk"), None, None, None),
        P(("shot", "blk")),
        P(),
        P(),
        P("shot"),
        P("shot", None),
        P("shot", "blk", None),
        P("shot", "blk", None, None),
        P("shot", "blk", None, None),
        P("shot", "blk", None, None),
        P("shot", "blk", None, None),
        P("shot", "blk", None, None),
    )
    out_specs = (
        P(("shot", "blk"), None, None, None),
        P("shot", "blk", None, None),
        P("shot", "blk", None, None),
    )

    return jax.shard_map(local, mesh=mesh, in_specs=in_specs, out_specs=out_specs, check_vma=False)
```
